512 devices in a mesh: ctx: 64 (over y, x, z_hi), head: 8 (over z_lo, core).
Axes of the slice: x: 4, y: 8, z: 8 (z_hi: 2, z_lo: 4; z = z_hi * 4 + z_lo), core: 2. Of those that a mesh axis runs over, the one named last changes fastest.
Arguments:
- head_inputs: bfloat16 [8192, 2048], P('ctx', 'head'), may hold values from -0.125 to 0.125
- write_keys: bfloat16 [8192, 128], P('ctx'), may hold values from -0.1875 to 0.1875
- read_queries: bfloat16 [8192, 128], P('ctx'), may hold values from -0.1875 to 0.1875
- log_decay: float32 [64, 8192], P('head', 'ctx'), may hold values from -1 to 0, as said below
- out_grad: bfloat16 [8192, 2048], P('ctx', 'head'), may hold values from -16 to 16
Outputs:
- input_grad: bfloat16 [8192, 2048], P('ctx', 'head')
- write_grad: bfloat16 [8192, 128], P(('ctx', 'head'))
- read_grad: bfloat16 [8192, 128], P(('ctx', 'head'))
The draws below stay inside these ranges and needn't reach their ends.
Inputs may be any that keep to these rules, and one draw needn't show every extreme that they name: `log_decay`: negative everywhere.
All inputs are finite; a program needn't handle non-finite values.
Results may differ from the reference program's by a relative error of at most 0.0063.
Values sent between devices are 32-bit elements; how exact they have to be, the bound alone decides.
No kernel may reach another device: no remote copies, remote signals or barrier semaphores. Data moves between devices by JAX's collectives and lax.ppermute only.
A program may use at most 64 MiB of HBM per device.

```python
import math
import jax
import jax.numpy as jnp
from jax import lax

HEAD_TOTAL = 64
P_SIZE = 32
N = 128
L = 128
TOK_DEV = 128
SEQUENCE_LENGTH = 8192


def draw_log_decay(key, part):
    random_subkeys = jax.random.split(key, 7)
    quick_share = 0.5
    quick_head = jax.random.bernoulli(random_subkeys[0], quick_share, (HEAD_TOTAL, 1))
    quick_rate = jnp.exp(jax.random.uniform(random_subkeys[1], (HEAD_TOTAL, 1), jnp.float32, math.log(1.0 / 50.0), math.log(1.0 / 30.0)))
    retained = jnp.exp(jax.random.uniform(random_subkeys[2], (HEAD_TOTAL, 1), jnp.float32, math.log(0.4), math.log(0.9)))
    slow_rate = -jnp.log(retained) / SEQUENCE_LENGTH
    decay_speed = jnp.where(quick_head, quick_rate, slow_rate)
    block_total = SEQUENCE_LENGTH // TOK_DEV
    block_factor = jnp.exp(jax.random.uniform(random_subkeys[3], (HEAD_TOTAL, block_total, 1), jnp.float32, math.log(0.5), math.log(2.0)))
    block_factor = jnp.broadcast_to(block_factor, (HEAD_TOTAL, block_total, TOK_DEV)).reshape(HEAD_TOTAL, SEQUENCE_LENGTH)
    jaggedness = jax.random.uniform(random_subkeys[4], (HEAD_TOTAL, SEQUENCE_LENGTH), jnp.float32, 0.4, 1.6)
    spike_mask = jax.random.bernoulli(random_subkeys[5], 2.0 / SEQUENCE_LENGTH, (HEAD_TOTAL, SEQUENCE_LENGTH)).astype(jnp.float32)
    spike_loss = spike_mask * jax.random.uniform(random_subkeys[6], (HEAD_TOTAL, SEQUENCE_LENGTH), jnp.float32, 0.22, 0.51)
    return -(decay_speed * block_factor * jaggedness) - spike_loss


def spiked(result, own_key, source, target, parts, factor):
    def block_of(axis_at):
        return (jnp.arange(result.shape[axis_at]) // (result.shape[axis_at] // parts)).reshape((-1,) + (1,) * (result.ndim - 1 - axis_at))

    one_side = jax.random.permutation(own_key, parts)[block_of(target)]
    other_side = (block_of(target) + parts // 2) % parts
    return jnp.where((block_of(source) == one_side) | (block_of(source) == other_side), factor * result, result)


def levels(rng, extent, cuts, least, largest):
    level, own = 1.0, jax.random.fold_in(rng, 6)
    for dim, blocks in cuts:
        draws = jnp.exp(jax.random.uniform(jax.random.fold_in(own, dim), (blocks,), jnp.float32, least / len(cuts), largest / len(cuts)))
        level = level * jnp.repeat(draws, extent[dim] // blocks).reshape([-1 if axis == dim else 1 for axis in range(len(extent))])
    return level


def normal_values(own_key, shape, deviation, reach, pieces=(), dtype=jnp.bfloat16):
    result = jax.random.normal(own_key, shape, jnp.float32) * deviation
    if len(pieces) > 0:
        result = levels(own_key, shape, pieces, -0.22, 0.18) * result
    return jnp.clip(result, min=-reach, max=reach).astype(dtype)


def noise_with(rng, dims, scale, most, cuts, heavy, dtype=jnp.bfloat16):
    result = scale * jax.random.normal(rng, dims, jnp.float32)
    if cuts:
        result = result * levels(rng, dims, cuts, -0.22, 0.18)
    return jnp.clip(spiked(result, jax.random.fold_in(rng, 3), *heavy), -most, most).astype(dtype)


def setup_inputs(seed: int = 0) -> dict:
    seeds = jax.random.split(jax.random.key(seed), 6)
    return {
        "head_inputs": noise_with(seeds[0], (SEQUENCE_LENGTH, HEAD_TOTAL * P_SIZE), 0.0078125, 0.125, ((0, 64), (1, 8)), (1, 0, 64, 4.0)),
        "write_keys": normal_values(seeds[1], (SEQUENCE_LENGTH, N), 0.03125, 0.1875, ((0, 64),)),
        "read_queries": normal_values(seeds[2], (SEQUENCE_LENGTH, N), 0.03125, 0.1875, ((0, 64),)),
        "log_decay": draw_log_decay(jax.random.fold_in(seeds[5], 71), 0),
        "out_grad": noise_with(seeds[4], (SEQUENCE_LENGTH, HEAD_TOTAL * P_SIZE), 1.0, 16.0, ((0, 64), (1, 8)), (1, 0, 64, 4.0)),
    }


def decay_table(cumulative):
    length = cumulative.shape[1]
    causal = jnp.arange(length)[:, None] >= jnp.arange(length)[None, :]
    spread = cumulative[:, :, None] - cumulative[:, None, :]
    return jnp.exp(jnp.where(causal[None], spread, -jnp.inf))


def scaled_rows(values, factor):
    head_count = factor.shape[0]
    length = factor.shape[1]
    shaped = values.astype(jnp.float32).reshape(length, head_count, -1) * factor.T[:, :, None]
    return shaped.astype(jnp.bfloat16).reshape(length, -1)


def reference(head_inputs, write_keys, read_queries, log_decay, out_grad):
    block_count = SEQUENCE_LENGTH // L
    feature_width = HEAD_TOTAL * P_SIZE
    cumulative = jnp.cumsum(log_decay.reshape(HEAD_TOTAL, block_count, L), axis=2).transpose(1, 0, 2)
    inputs_blk = head_inputs.reshape(block_count, L, feature_width)
    grads_blk = out_grad.reshape(block_count, L, feature_width)
    write_blk = write_keys.reshape(block_count, L, N)
    read_blk = read_queries.reshape(block_count, L, N)
    empty_state = jnp.zeros((N, feature_width), jnp.float32)

    def backward_step(current, element):
        block_grads, block_read, block_cum = element
        weighted_grads = scaled_rows(block_grads, jnp.exp(block_cum))
        through = jnp.repeat(jnp.exp(block_cum[:, -1]), P_SIZE)
        own_grad = jnp.dot(block_read.T, weighted_grads, preferred_element_type=jnp.float32)
        return own_grad + through[None, :] * current, current.astype(jnp.bfloat16)

    _, exits_bf = lax.scan(backward_step, empty_state, (grads_blk, read_blk, cumulative), reverse=True)

    def forward_step(current, element):
        block_inputs, block_grads, block_write, block_read, block_cum, exit_bf = element
        decay_mat = decay_table(block_cum)
        scores = jnp.dot(block_read, block_write.T, preferred_element_type=jnp.float32)
        mixing = (scores[None] * decay_mat).astype(jnp.bfloat16)
        inputs_heads = block_inputs.astype(jnp.float32).reshape(L, HEAD_TOTAL, P_SIZE)
        grads_heads = block_grads.astype(jnp.float32).reshape(L, HEAD_TOTAL, P_SIZE)
        input_mix = jnp.einsum("hts,thp->shp", mixing.astype(jnp.float32), grads_heads).reshape(L, feature_width)
        pair_grad = jnp.einsum("thp,shp->hts", grads_heads, inputs_heads)
        score_grad = jnp.sum(pair_grad * decay_mat, axis=0)
        block_end = block_cum[:, -1:]
        forward_w = jnp.exp(block_end - block_cum)
        weighted_inputs = scaled_rows(block_inputs, forward_w)
        weighted_grads = scaled_rows(block_grads, jnp.exp(block_cum))
        entry_bf = current.astype(jnp.bfloat16)
        input_state = jnp.dot(block_write, exit_bf, preferred_element_type=jnp.float32).reshape(L, HEAD_TOTAL, P_SIZE) * forward_w.T[:, :, None]
        input_grad = (input_mix + input_state.reshape(L, feature_width)).astype(jnp.bfloat16)
        write_grad = jnp.dot(score_grad.T, block_read.astype(jnp.float32), precision=lax.Precision.HIGHEST)
        write_grad = write_grad + jnp.dot(weighted_inputs, exit_bf.T, preferred_element_type=jnp.float32)
        read_grad = jnp.dot(score_grad, block_write.astype(jnp.float32), precision=lax.Precision.HIGHEST)
        read_grad = read_grad + jnp.dot(weighted_grads, entry_bf.T, preferred_element_type=jnp.float32)
        through = jnp.repeat(jnp.exp(block_end[:, 0]), P_SIZE)
        own_state = jnp.dot(block_write.T, weighted_inputs, preferred_element_type=jnp.float32)
        following = through[None, :] * current + own_state
        return following, (input_grad, write_grad.astype(jnp.bfloat16), read_grad.astype(jnp.bfloat16))

    _, outputs = lax.scan(forward_step, empty_state, (inputs_blk, grads_blk, write_blk, read_blk, cumulative, exits_bf))
    input_all, write_all, read_all = outputs
    return input_all.reshape(SEQUENCE_LENGTH, feature_width), write_all.reshape(SEQUENCE_LENGTH, N), read_all.reshape(SEQUENCE_LENGTH, N)
```

```python
import jax
import jax.numpy as jnp
from jax import lax
from jax.sharding import PartitionSpec as P


def scan_exclusive(decay, state, axis, reverse):
    devices, mine = lax.axis_size(axis), lax.axis_index(axis)
    window = jnp.concatenate([decay[None, :], state], axis=0)
    outer_decay = jnp.ones_like(decay)
    outer_state = jnp.zeros_like(state)
    shift = 1
    while shift < devices:
        if reverse:
            pairs = [(i + shift, i) for i in range(devices - shift)]
            valid = mine < devices - shift
        else:
            pairs = [(i, i + shift) for i in range(devices - shift)]
            valid = mine >= shift
        got = lax.ppermute(window, axis, pairs)
        got_decay, got_state = got[0], got[1:]
        outer_state = outer_decay[None, :] * got_state + outer_state
        outer_decay = jnp.where(valid, got_decay * outer_decay, outer_decay)
        shift *= 2
        if shift < devices:
            win_decay, win_state = window[0], window[1:]
            new_state = win_decay[None, :] * got_state + win_state
            new_decay = jnp.where(valid, got_decay * win_decay, win_decay)
            window = jnp.concatenate([new_decay[None, :], new_state], axis=0)
    return outer_state


def heads_scaled(values, factor):
    head_count, length = factor.shape
    shaped = values.astype(jnp.float32).reshape(length, head_count, -1) * factor.T[:, :, None]
    return shaped.astype(jnp.bfloat16).reshape(length, -1)


def per_device(head_inputs, write_keys, read_queries, log_decay, out_grad):
    length, feature_width = head_inputs.shape
    head_count = log_decay.shape[0]
    head_size = feature_width // head_count
    cumulative = jnp.cumsum(log_decay, axis=1)
    block_end = cumulative[:, -1:]
    forward_w = jnp.exp(block_end - cumulative)
    backward_w = jnp.exp(cumulative)
    weighted_inputs = heads_scaled(head_inputs, forward_w)
    weighted_grads = heads_scaled(out_grad, backward_w)
    through = jnp.repeat(jnp.exp(block_end[:, 0]), head_size)
    own_state = jnp.dot(write_keys.T, weighted_inputs, preferred_element_type=jnp.float32)
    own_grad = jnp.dot(read_queries.T, weighted_grads, preferred_element_type=jnp.float32)

    entry = scan_exclusive(through, own_state, "ctx", reverse=False)
    exit_ = scan_exclusive(through, own_grad, "ctx", reverse=True)
    entry_bf = entry.astype(jnp.bfloat16)
    exit_bf = exit_.astype(jnp.bfloat16)

    causal = jnp.arange(length)[:, None] >= jnp.arange(length)[None, :]
    spread = cumulative[:, :, None] - cumulative[:, None, :]
    decay_mat = jnp.exp(jnp.where(causal[None], spread, -jnp.inf))
    scores = jnp.dot(read_queries, write_keys.T, preferred_element_type=jnp.float32)
    mixing = (scores[None] * decay_mat).astype(jnp.bfloat16)
    inputs_heads = head_inputs.reshape(length, head_count, head_size)
    grads_heads = out_grad.reshape(length, head_count, head_size)
    input_mix = jnp.einsum(
        "hts,thp->shp", mixing, grads_heads, preferred_element_type=jnp.float32
    )
    pair_grad = jnp.einsum(
        "thp,shp->hts", grads_heads, inputs_heads, preferred_element_type=jnp.float32
    )
    score_grad = jnp.sum(pair_grad * decay_mat, axis=0)
    write_mix = jnp.dot(
        score_grad.T, read_queries.astype(jnp.float32), precision=lax.Precision.HIGHEST
    )
    read_mix = jnp.dot(
        score_grad, write_keys.astype(jnp.float32), precision=lax.Precision.HIGHEST
    )

    input_state = (
        jnp.dot(write_keys, exit_bf, preferred_element_type=jnp.float32).reshape(
            length, head_count, head_size
        )
        * forward_w.T[:, :, None]
    )
    input_grad = (input_mix + input_state).astype(jnp.bfloat16).reshape(length, feature_width)
    write_state = jnp.dot(weighted_inputs, exit_bf.T, preferred_element_type=jnp.float32)
    read_state = jnp.dot(weighted_grads, entry_bf.T, preferred_element_type=jnp.float32)
    both = jnp.concatenate([write_mix + write_state, read_mix + read_state], axis=1)
    summed = lax.psum_scatter(both, "head", scatter_dimension=0, tiled=True)
    states = write_keys.shape[1]
    write_sum, read_sum = summed[:, :states], summed[:, states:]
    return (input_grad, write_sum.astype(jnp.bfloat16), read_sum.astype(jnp.bfloat16))


def solution(mesh):
    placed = (P("ctx", "head"), P("ctx", None), P("ctx", None), P("head", "ctx"), P("ctx", "head"))
    return jax.shard_map(
        per_device,
        mesh=mesh,
        in_specs=placed,
        out_specs=(P("ctx", "head"), P(("ctx", "head"), None), P(("ctx", "head"), None)),
        check_vma=False,
    )
```

```python
import jax
import jax.numpy as jnp
from jax import lax
from jax.sharding import PartitionSpec as P


def scan_both(decay, state, grad, axis):
    devices, mine = lax.axis_size(axis), lax.axis_index(axis)
    block_decay, block_state, block_grad = decay, state, grad
    prefix_decay, prefix_state = jnp.ones_like(decay), jnp.zeros_like(state)
    suffix_decay, suffix_grad = jnp.ones_like(decay), jnp.zeros_like(grad)
    rows = state.shape[0]
    shift = 1
    while shift < devices:
        pairs = [(i, i ^ shift) for i in range(devices)]
        message = jnp.concatenate([block_decay[None, :], block_state, block_grad], axis=0)
        got = lax.ppermute(message, axis, pairs)
        got_decay, got_state, got_grad = got[0], got[1 : rows + 1], got[rows + 1 :]
        later = (mine & shift) != 0
        prefix_state = jnp.where(later, prefix_decay[None, :] * got_state + prefix_state, prefix_state)
        prefix_decay = jnp.where(later, got_decay * prefix_decay, prefix_decay)
        suffix_grad = jnp.where(later, suffix_grad, suffix_decay[None, :] * got_grad + suffix_grad)
        suffix_decay = jnp.where(later, suffix_decay, got_decay * suffix_decay)
        shift *= 2
        if shift < devices:
            block_state = jnp.where(
                later,
                block_decay[None, :] * got_state + block_state,
                got_decay[None, :] * block_state + got_state,
            )
            block_grad = jnp.where(
                later,
                got_decay[None, :] * block_grad + got_grad,
                block_decay[None, :] * got_grad + block_grad,
            )
            block_decay = got_decay * block_decay
    return prefix_state, suffix_grad


def scatter_sum(values, axis):
    devices, mine = lax.axis_size(axis), lax.axis_index(axis)
    bits = devices.bit_length() - 1
    rows, cols = values.shape
    piece = rows // devices
    x = values.reshape((2,) * bits + (piece, cols))
    x = x.transpose(tuple(range(bits - 1, -1, -1)) + (bits, bits + 1)).reshape(rows, cols)
    shift = 1
    while shift < devices:
        half = x.shape[0] // 2
        upper = (mine & shift) != 0
        keep = jnp.where(upper, x[half:], x[:half])
        send = jnp.where(upper, x[:half], x[half:])
        got = lax.ppermute(send, axis, [(i, i ^ shift) for i in range(devices)])
        x = keep + got
        shift *= 2
    return x


def heads_scaled(values, factor):
    head_count, length = factor.shape
    shaped = values.astype(jnp.float32).reshape(length, head_count, -1) * factor.T[:, :, None]
    return shaped.astype(jnp.bfloat16).reshape(length, -1)


def per_device(head_inputs, write_keys, read_queries, log_decay, out_grad):
    length, feature_width = head_inputs.shape
    head_count = log_decay.shape[0]
    head_size = feature_width // head_count
    cumulative = jnp.cumsum(log_decay, axis=1)
    block_end = cumulative[:, -1:]
    forward_w = jnp.exp(block_end - cumulative)
    backward_w = jnp.exp(cumulative)
    weighted_inputs = heads_scaled(head_inputs, forward_w)
    weighted_grads = heads_scaled(out_grad, backward_w)
    through = jnp.repeat(jnp.exp(block_end[:, 0]), head_size)
    own_state = jnp.dot(write_keys.T, weighted_inputs, preferred_element_type=jnp.float32)
    own_grad = jnp.dot(read_queries.T, weighted_grads, preferred_element_type=jnp.float32)

    entry, exit_ = scan_both(through, own_state, own_grad, "ctx")
    entry_bf = entry.astype(jnp.bfloat16)
    exit_bf = exit_.astype(jnp.bfloat16)

    causal = jnp.arange(length)[:, None] >= jnp.arange(length)[None, :]
    spread = cumulative[:, :, None] - cumulative[:, None, :]
    decay_mat = jnp.exp(jnp.where(causal[None], spread, -jnp.inf))
    scores = jnp.dot(read_queries, write_keys.T, preferred_element_type=jnp.float32)
    mixing = (scores[None] * decay_mat).astype(jnp.bfloat16)
    inputs_heads = head_inputs.reshape(length, head_count, head_size)
    grads_heads = out_grad.reshape(length, head_count, head_size)
    input_mix = jnp.einsum(
        "hts,thp->shp", mixing, grads_heads, preferred_element_type=jnp.float32
    )
    pair_grad = jnp.einsum(
        "thp,shp->hts", grads_heads, inputs_heads, preferred_element_type=jnp.float32
    )
    score_grad = jnp.sum(pair_grad * decay_mat, axis=0)
    write_mix = jnp.dot(
        score_grad.T, read_queries.astype(jnp.float32), precision=lax.Precision.HIGHEST
    )
    read_mix = jnp.dot(
        score_grad, write_keys.astype(jnp.float32), precision=lax.Precision.HIGHEST
    )

    input_state = (
        jnp.dot(write_keys, exit_bf, preferred_element_type=jnp.float32).reshape(
            length, head_count, head_size
        )
        * forward_w.T[:, :, None]
    )
    input_grad = (input_mix + input_state).astype(jnp.bfloat16).reshape(length, feature_width)
    write_state = jnp.dot(weighted_inputs, exit_bf.T, preferred_element_type=jnp.float32)
    read_state = jnp.dot(weighted_grads, entry_bf.T, preferred_element_type=jnp.float32)
    both = jnp.concatenate([write_mix + write_state, read_mix + read_state], axis=1)
    summed = scatter_sum(both, "head")
    states = write_keys.shape[1]
    write_sum, read_sum = summed[:, :states], summed[:, states:]
    return (input_grad, write_sum.astype(jnp.bfloat16), read_sum.astype(jnp.bfloat16))


def solution(mesh):
    placed = (P("ctx", "head"), P("ctx", None), P("ctx", None), P("head", "ctx"), P("ctx", "head"))
    return jax.shard_map(
        per_device,
        mesh=mesh,
        in_specs=placed,
        out_specs=(P("ctx", "head"), P(("ctx", "head"), None), P(("ctx", "head"), None)),
        check_vma=False,
    )
```

```python
import functools

import jax
import jax.numpy as jnp
from jax import lax
from jax.sharding import PartitionSpec as P


def joined(earlier, later):
    a1, s1, g1 = earlier
    a2, s2, g2 = later
    return (a1 * a2, a2[None, :] * s1 + s2, a1[None, :] * g2 + g1)


def chosen(flag, yes, no):
    return tuple(jnp.where(flag, y, n) for y, n in zip(yes, no))


def scan_groups(decay, state, grad, axes):
    rows = state.shape[0]
    identity = (jnp.ones_like(decay), jnp.zeros_like(state), jnp.zeros_like(grad))
    block = (decay, state, grad)
    prefix, suffix = identity, identity
    for at, axis in enumerate(axes):
        size, mine = lax.axis_size(axis), lax.axis_index(axis)
        message = jnp.concatenate([block[0][None, :], block[1], block[2]], axis=0)
        spread = jnp.broadcast_to(message[None], (size,) + message.shape)
        got = lax.all_to_all(spread, axis, 0, 0)
        before, after, total = identity, identity, identity
        for member in range(size):
            piece = (got[member, 0], got[member, 1 : rows + 1], got[member, rows + 1 :])
            before = chosen(member < mine, joined(before, piece), before)
            after = chosen(member > mine, joined(after, piece), after)
            if at + 1 < len(axes):
                total = joined(total, piece)
        prefix = joined(before, prefix)
        suffix = joined(suffix, after)
        block = total
    return prefix[1], suffix[2]


def scatter_sum(values, axis):
    devices = lax.axis_size(axis)
    rows, cols = values.shape
    got = lax.all_to_all(values.reshape(devices, rows // devices, cols), axis, 0, 0)
    return jnp.sum(got, axis=0)


def heads_scaled(values, factor):
    head_count, length = factor.shape
    shaped = values.astype(jnp.float32).reshape(length, head_count, -1) * factor.T[:, :, None]
    return shaped.astype(jnp.bfloat16).reshape(length, -1)


def per_device(ctx_parts, head_inputs, write_keys, read_queries, log_decay, out_grad):
    length, feature_width = head_inputs.shape
    head_count = log_decay.shape[0]
    head_size = feature_width // head_count
    cumulative = jnp.cumsum(log_decay, axis=1)
    block_end = cumulative[:, -1:]
    forward_w = jnp.exp(block_end - cumulative)
    backward_w = jnp.exp(cumulative)
    weighted_inputs = heads_scaled(head_inputs, forward_w)
    weighted_grads = heads_scaled(out_grad, backward_w)
    through = jnp.repeat(jnp.exp(block_end[:, 0]), head_size)
    own_state = jnp.dot(write_keys.T, weighted_inputs, preferred_element_type=jnp.float32)
    own_grad = jnp.dot(read_queries.T, weighted_grads, preferred_element_type=jnp.float32)

    entry, exit_ = scan_groups(through, own_state, own_grad, ctx_parts[::-1])
    entry_bf = entry.astype(jnp.bfloat16)
    exit_bf = exit_.astype(jnp.bfloat16)

    causal = jnp.arange(length)[:, None] >= jnp.arange(length)[None, :]
    spread = cumulative[:, :, None] - cumulative[:, None, :]
    decay_mat = jnp.exp(jnp.where(causal[None], spread, -jnp.inf))
    scores = jnp.dot(read_queries, write_keys.T, preferred_element_type=jnp.float32)
    mixing = (scores[None] * decay_mat).astype(jnp.bfloat16)
    inputs_heads = head_inputs.reshape(length, head_count, head_size)
    grads_heads = out_grad.reshape(length, head_count, head_size)
    input_mix = jnp.einsum(
        "hts,thp->shp", mixing, grads_heads, preferred_element_type=jnp.float32
    )
    pair_grad = jnp.einsum(
        "thp,shp->hts", grads_heads, inputs_heads, preferred_element_type=jnp.float32
    )
    score_grad = jnp.sum(pair_grad * decay_mat, axis=0)
    write_mix = jnp.dot(
        score_grad.T, read_queries.astype(jnp.float32), precision=lax.Precision.HIGHEST
    )
    read_mix = jnp.dot(
        score_grad, write_keys.astype(jnp.float32), precision=lax.Precision.HIGHEST
    )

    input_state = (
        jnp.dot(write_keys, exit_bf, preferred_element_type=jnp.float32).reshape(
            length, head_count, head_size
        )
        * forward_w.T[:, :, None]
    )
    input_grad = (input_mix + input_state).astype(jnp.bfloat16).reshape(length, feature_width)
    write_state = jnp.dot(weighted_inputs, exit_bf.T, preferred_element_type=jnp.float32)
    read_state = jnp.dot(weighted_grads, entry_bf.T, preferred_element_type=jnp.float32)
    both = jnp.concatenate([write_mix + write_state, read_mix + read_state], axis=1)
    summed = scatter_sum(both, "head")
    states = write_keys.shape[1]
    write_sum, read_sum = summed[:, :states], summed[:, states:]
    return (input_grad, write_sum.astype(jnp.bfloat16), read_sum.astype(jnp.bfloat16))


def solution(mesh):
    ctx_size = mesh.shape["ctx"]
    radix = 4
    sizes = []
    while ctx_size > 1:
        sizes.append(min(radix, ctx_size))
        ctx_size //= sizes[-1]
    parts = tuple("c%d" % i for i in range(len(sizes)))[::-1]
    devices = mesh.devices.reshape(tuple(sizes[::-1]) + (mesh.shape["head"],))
    split = jax.sharding.Mesh(devices, parts + ("head",))
    placed = (P(parts, "head"), P(parts, None), P(parts, None), P("head", parts), P(parts, "head"))
    return jax.shard_map(
        functools.partial(per_device, parts),
        mesh=split,
        in_specs=placed,
        out_specs=(P(parts, "head"), P(parts + ("head",), None), P(parts + ("head",), None)),
        check_vma=False,
    )
```

```python
import functools

import jax
import jax.numpy as jnp
from jax import lax
from jax.sharding import PartitionSpec as P


def joined(earlier, later):
    a1, s1, g1 = earlier
    a2, s2, g2 = later
    return (a1 * a2, a2[None, :] * s1 + s2, a1[None, :] * g2 + g1)


def chosen(flag, yes, no):
    return tuple(jnp.where(flag, y, n) for y, n in zip(yes, no))


def scan_groups(decay, state, grad, axis, widths):
    devices, mine = lax.axis_size(axis), lax.axis_index(axis)
    rows = state.shape[0]
    identity = (jnp.ones_like(decay), jnp.zeros_like(state), jnp.zeros_like(grad))
    block = (decay, state, grad)
    prefix, suffix = identity, identity
    low = 0
    for at, width in enumerate(widths):
        size = 1 << width
        place = (mine >> low) & (size - 1)
        message = jnp.concatenate([block[0][None, :], block[1], block[2]], axis=0)
        got = {0: message}
        for offset in range(1, size):
            flip = offset << low
            got[offset] = lax.ppermute(message, axis, [(i, i ^ flip) for i in range(devices)])
        before, after, total = identity, identity, identity
        for member in range(size):
            offset_of = place ^ member
            arrived = got[0]
            for offset in range(1, size):
                arrived = jnp.where(offset_of == offset, got[offset], arrived)
            piece = (arrived[0], arrived[1 : rows + 1], arrived[rows + 1 :])
            before = chosen(member < place, joined(before, piece), before)
            after = chosen(member > place, joined(after, piece), after)
            if at + 1 < len(widths):
                total = joined(total, piece)
        prefix = joined(before, prefix)
        suffix = joined(suffix, after)
        block = total
        low += width
    return prefix[1], suffix[2]


def scatter_sum(values, axis):
    devices = lax.axis_size(axis)
    rows, cols = values.shape
    got = lax.all_to_all(values.reshape(devices, rows // devices, cols), axis, 0, 0)
    return jnp.sum(got, axis=0)


def heads_scaled(values, factor):
    head_count, length = factor.shape
    shaped = values.astype(jnp.float32).reshape(length, head_count, -1) * factor.T[:, :, None]
    return shaped.astype(jnp.bfloat16).reshape(length, -1)


def per_device(widths, head_inputs, write_keys, read_queries, log_decay, out_grad):
    length, feature_width = head_inputs.shape
    head_count = log_decay.shape[0]
    head_size = feature_width // head_count
    cumulative = jnp.cumsum(log_decay, axis=1)
    block_end = cumulative[:, -1:]
    forward_w = jnp.exp(block_end - cumulative)
    backward_w = jnp.exp(cumulative)
    weighted_inputs = heads_scaled(head_inputs, forward_w)
    weighted_grads = heads_scaled(out_grad, backward_w)
    through = jnp.repeat(jnp.exp(block_end[:, 0]), head_size)
    own_state = jnp.dot(write_keys.T, weighted_inputs, preferred_element_type=jnp.float32)
    own_grad = jnp.dot(read_queries.T, weighted_grads, preferred_element_type=jnp.float32)

    entry, exit_ = scan_groups(through, own_state, own_grad, "ctx", widths)
    entry_bf = entry.astype(jnp.bfloat16)
    exit_bf = exit_.astype(jnp.bfloat16)

    causal = jnp.arange(length)[:, None] >= jnp.arange(length)[None, :]
    spread = cumulative[:, :, None] - cumulative[:, None, :]
    decay_mat = jnp.exp(jnp.where(causal[None], spread, -jnp.inf))
    scores = jnp.dot(read_queries, write_keys.T, preferred_element_type=jnp.float32)
    mixing = (scores[None] * decay_mat).astype(jnp.bfloat16)
    inputs_heads = head_inputs.reshape(length, head_count, head_size)
    grads_heads = out_grad.reshape(length, head_count, head_size)
    input_mix = jnp.einsum(
        "hts,thp->shp", mixing, grads_heads, preferred_element_type=jnp.float32
    )
    pair_grad = jnp.einsum(
        "thp,shp->hts", grads_heads, inputs_heads, preferred_element_type=jnp.float32
    )
    score_grad = jnp.sum(pair_grad * decay_mat, axis=0)
    write_mix = jnp.dot(
        score_grad.T, read_queries.astype(jnp.float32), precision=lax.Precision.HIGHEST
    )
    read_mix = jnp.dot(
        score_grad, write_keys.astype(jnp.float32), precision=lax.Precision.HIGHEST
    )

    input_state = (
        jnp.dot(write_keys, exit_bf, preferred_element_type=jnp.float32).reshape(
            length, head_count, head_size
        )
        * forward_w.T[:, :, None]
    )
    input_grad = (input_mix + input_state).astype(jnp.bfloat16).reshape(length, feature_width)
    write_state = jnp.dot(weighted_inputs, exit_bf.T, preferred_element_type=jnp.float32)
    read_state = jnp.dot(weighted_grads, entry_bf.T, preferred_element_type=jnp.float32)
    both = jnp.concatenate([write_mix + write_state, read_mix + read_state], axis=1)
    summed = scatter_sum(both, "head")
    states = write_keys.shape[1]
    write_sum, read_sum = summed[:, :states], summed[:, states:]
    return (input_grad, write_sum.astype(jnp.bfloat16), read_sum.astype(jnp.bfloat16))


SCAN_WIDTHS = (2, 2, 2)


def solution(mesh):
    bits = mesh.shape["ctx"].bit_length() - 1
    widths, left = [], bits
    for width in SCAN_WIDTHS:
        if left > 0:
            widths.append(min(width, left))
            left -= widths[-1]
    while left > 0:
        widths.append(1)
        left -= 1
    placed = (P("ctx", "head"), P("ctx", None), P("ctx", None), P("head", "ctx"), P("ctx", "head"))
    return jax.shard_map(
        functools.partial(per_device, tuple(widths)),
        mesh=mesh,
        in_specs=placed,
        out_specs=(P("ctx", "head"), P(("ctx", "head"), None), P(("ctx", "head"), None)),
        check_vma=False,
    )
```

```python
import jax
import jax.numpy as jnp
from jax import lax
from jax.sharding import PartitionSpec as P


def scan_both(decay, state, grad, axis):
    devices, mine = lax.axis_size(axis), lax.axis_index(axis)
    block_decay, block_state, block_grad = decay, state, grad
    prefix_decay, prefix_state = jnp.ones_like(decay), jnp.zeros_like(state)
    suffix_decay, suffix_grad = jnp.ones_like(decay), jnp.zeros_like(grad)
    rows = state.shape[0]
    shift = 1
    while shift < devices:
        pairs = [(i, i ^ shift) for i in range(devices)]
        later = (mine & shift) != 0
        last = shift * 2 >= devices
        if last:
            message = jnp.concatenate(
                [block_decay[None, :], jnp.where(later, block_grad, block_state)], axis=0
            )
            got = lax.ppermute(message, axis, pairs)
            got_decay, got_state, got_grad = got[0], got[1:], got[1:]
        else:
            message = jnp.concatenate([block_decay[None, :], block_state, block_grad], axis=0)
            got = lax.ppermute(message, axis, pairs)
            got_decay, got_state, got_grad = got[0], got[1 : rows + 1], got[rows + 1 :]
        prefix_state = jnp.where(later, prefix_decay[None, :] * got_state + prefix_state, prefix_state)
        prefix_decay = jnp.where(later, got_decay * prefix_decay, prefix_decay)
        suffix_grad = jnp.where(later, suffix_grad, suffix_decay[None, :] * got_grad + suffix_grad)
        suffix_decay = jnp.where(later, suffix_decay, got_decay * suffix_decay)
        shift *= 2
        if not last:
            block_state = jnp.where(
                later,
                block_decay[None, :] * got_state + block_state,
                got_decay[None, :] * block_state + got_state,
            )
            block_grad = jnp.where(
                later,
                got_decay[None, :] * block_grad + got_grad,
                block_decay[None, :] * got_grad + block_grad,
            )
            block_decay = got_decay * block_decay
    return prefix_state, suffix_grad


def scatter_sum(values, axis):
    devices = lax.axis_size(axis)
    rows, cols = values.shape
    got = lax.all_to_all(values.reshape(devices, rows // devices, cols), axis, 0, 0)
    return jnp.sum(got, axis=0)


def heads_scaled(values, factor):
    head_count, length = factor.shape
    shaped = values.astype(jnp.float32).reshape(length, head_count, -1) * factor.T[:, :, None]
    return shaped.astype(jnp.bfloat16).reshape(length, -1)


def per_device(head_inputs, write_keys, read_queries, log_decay, out_grad):
    length, feature_width = head_inputs.shape
    head_count = log_decay.shape[0]
    head_size = feature_width // head_count
    cumulative = jnp.cumsum(log_decay, axis=1)
    block_end = cumulative[:, -1:]
    forward_w = jnp.exp(block_end - cumulative)
    backward_w = jnp.exp(cumulative)
    weighted_inputs = heads_scaled(head_inputs, forward_w)
    weighted_grads = heads_scaled(out_grad, backward_w)
    through = jnp.repeat(jnp.exp(block_end[:, 0]), head_size)
    own_state = jnp.dot(write_keys.T, weighted_inputs, preferred_element_type=jnp.float32)
    own_grad = jnp.dot(read_queries.T, weighted_grads, preferred_element_type=jnp.float32)

    entry, exit_ = scan_both(through, own_state, own_grad, "ctx")
    entry_bf = entry.astype(jnp.bfloat16)
    exit_bf = exit_.astype(jnp.bfloat16)

    causal = jnp.arange(length)[:, None] >= jnp.arange(length)[None, :]
    spread = cumulative[:, :, None] - cumulative[:, None, :]
    decay_mat = jnp.exp(jnp.where(causal[None], spread, -jnp.inf))
    scores = jnp.dot(read_queries, write_keys.T, preferred_element_type=jnp.float32)
    mixing = (scores[None] * decay_mat).astype(jnp.bfloat16)
    inputs_heads = head_inputs.reshape(length, head_count, head_size)
    grads_heads = out_grad.reshape(length, head_count, head_size)
    input_mix = jnp.einsum(
        "hts,thp->shp", mixing, grads_heads, preferred_element_type=jnp.float32
    )
    pair_grad = jnp.einsum(
        "thp,shp->hts", grads_heads, inputs_heads, preferred_element_type=jnp.float32
    )
    score_grad = jnp.sum(pair_grad * decay_mat, axis=0)
    write_mix = jnp.dot(
        score_grad.T, read_queries.astype(jnp.float32), precision=lax.Precision.HIGHEST
    )
    read_mix = jnp.dot(
        score_grad, write_keys.astype(jnp.float32), precision=lax.Precision.HIGHEST
    )

    input_state = (
        jnp.dot(write_keys, exit_bf, preferred_element_type=jnp.float32).reshape(
            length, head_count, head_size
        )
        * forward_w.T[:, :, None]
    )
    input_grad = (input_mix + input_state).astype(jnp.bfloat16).reshape(length, feature_width)
    write_state = jnp.dot(weighted_inputs, exit_bf.T, preferred_element_type=jnp.float32)
    read_state = jnp.dot(weighted_grads, entry_bf.T, preferred_element_type=jnp.float32)
    both = jnp.concatenate([write_mix + write_state, read_mix + read_state], axis=1)
    summed = scatter_sum(both, "head")
    states = write_keys.shape[1]
    write_sum, read_sum = summed[:, :states], summed[:, states:]
    return (input_grad, write_sum.astype(jnp.bfloat16), read_sum.astype(jnp.bfloat16))


def solution(mesh):
    placed = (P("ctx", "head"), P("ctx", None), P("ctx", None), P("head", "ctx"), P("ctx", "head"))
    return jax.shard_map(
        per_device,
        mesh=mesh,
        in_specs=placed,
        out_specs=(P("ctx", "head"), P(("ctx", "head"), None), P(("ctx", "head"), None)),
        check_vma=False,
    )
```

```python
import jax
import jax.numpy as jnp
from jax import lax
from jax.sharding import PartitionSpec as P


PARTNER_MASKS = {64: {4: 6, 32: 56}}


def scan_both(decay, state, grad, axis):
    devices, mine = lax.axis_size(axis), lax.axis_index(axis)
    block_decay, block_state, block_grad = decay, state, grad
    prefix_decay, prefix_state = jnp.ones_like(decay), jnp.zeros_like(state)
    suffix_decay, suffix_grad = jnp.ones_like(decay), jnp.zeros_like(grad)
    rows = state.shape[0]
    shift = 1
    while shift < devices:
        mask = PARTNER_MASKS.get(devices, {}).get(shift, shift)
        pairs = [(i, i ^ mask) for i in range(devices)]
        later = (mine & shift) != 0
        last = shift * 2 >= devices
        if last:
            message = jnp.concatenate(
                [block_decay[None, :], jnp.where(later, block_grad, block_state)], axis=0
            )
            got = lax.ppermute(message, axis, pairs)
            got_decay, got_state, got_grad = got[0], got[1:], got[1:]
        else:
            message = jnp.concatenate([block_decay[None, :], block_state, block_grad], axis=0)
            got = lax.ppermute(message, axis, pairs)
            got_decay, got_state, got_grad = got[0], got[1 : rows + 1], got[rows + 1 :]
        prefix_state = jnp.where(later, prefix_decay[None, :] * got_state + prefix_state, prefix_state)
        prefix_decay = jnp.where(later, got_decay * prefix_decay, prefix_decay)
        suffix_grad = jnp.where(later, suffix_grad, suffix_decay[None, :] * got_grad + suffix_grad)
        suffix_decay = jnp.where(later, suffix_decay, got_decay * suffix_decay)
        shift *= 2
        if not last:
            block_state = jnp.where(
                later,
                block_decay[None, :] * got_state + block_state,
                got_decay[None, :] * block_state + got_state,
            )
            block_grad = jnp.where(
                later,
                got_decay[None, :] * block_grad + got_grad,
                block_decay[None, :] * got_grad + block_grad,
            )
            block_decay = got_decay * block_decay
    return prefix_state, suffix_grad


def scatter_sum(values, axis):
    devices = lax.axis_size(axis)
    rows, cols = values.shape
    got = lax.all_to_all(values.reshape(devices, rows // devices, cols), axis, 0, 0)
    return jnp.sum(got, axis=0)


def heads_scaled(values, factor):
    head_count, length = factor.shape
    shaped = values.astype(jnp.float32).reshape(length, head_count, -1) * factor.T[:, :, None]
    return shaped.astype(jnp.bfloat16).reshape(length, -1)


def per_device(head_inputs, write_keys, read_queries, log_decay, out_grad):
    length, feature_width = head_inputs.shape
    head_count = log_decay.shape[0]
    head_size = feature_width // head_count
    cumulative = jnp.cumsum(log_decay, axis=1)
    block_end = cumulative[:, -1:]
    forward_w = jnp.exp(block_end - cumulative)
    backward_w = jnp.exp(cumulative)
    weighted_inputs = heads_scaled(head_inputs, forward_w)
    weighted_grads = heads_scaled(out_grad, backward_w)
    through = jnp.repeat(jnp.exp(block_end[:, 0]), head_size)
    own_state = jnp.dot(write_keys.T, weighted_inputs, preferred_element_type=jnp.float32)
    own_grad = jnp.dot(read_queries.T, weighted_grads, preferred_element_type=jnp.float32)

    entry, exit_ = scan_both(through, own_state, own_grad, "ctx")
    entry_bf = entry.astype(jnp.bfloat16)
    exit_bf = exit_.astype(jnp.bfloat16)

    causal = jnp.arange(length)[:, None] >= jnp.arange(length)[None, :]
    spread = cumulative[:, :, None] - cumulative[:, None, :]
    decay_mat = jnp.exp(jnp.where(causal[None], spread, -jnp.inf))
    scores = jnp.dot(read_queries, write_keys.T, preferred_element_type=jnp.float32)
    mixing = (scores[None] * decay_mat).astype(jnp.bfloat16)
    inputs_heads = head_inputs.reshape(length, head_count, head_size)
    grads_heads = out_grad.reshape(length, head_count, head_size)
    input_mix = jnp.einsum(
        "hts,thp->shp", mixing, grads_heads, preferred_element_type=jnp.float32
    )
    pair_grad = jnp.einsum(
        "thp,shp->hts", grads_heads, inputs_heads, preferred_element_type=jnp.float32
    )
    score_grad = jnp.sum(pair_grad * decay_mat, axis=0)
    write_mix = jnp.dot(
        score_grad.T, read_queries.astype(jnp.float32), precision=lax.Precision.HIGHEST
    )
    read_mix = jnp.dot(
        score_grad, write_keys.astype(jnp.float32), precision=lax.Precision.HIGHEST
    )

    input_state = (
        jnp.dot(write_keys, exit_bf, preferred_element_type=jnp.float32).reshape(
            length, head_count, head_size
        )
        * forward_w.T[:, :, None]
    )
    input_grad = (input_mix + input_state).astype(jnp.bfloat16).reshape(length, feature_width)
    write_state = jnp.dot(weighted_inputs, exit_bf.T, preferred_element_type=jnp.float32)
    read_state = jnp.dot(weighted_grads, entry_bf.T, preferred_element_type=jnp.float32)
    both = jnp.concatenate([write_mix + write_state, read_mix + read_state], axis=1)
    summed = scatter_sum(both, "head")
    states = write_keys.shape[1]
    write_sum, read_sum = summed[:, :states], summed[:, states:]
    return (input_grad, write_sum.astype(jnp.bfloat16), read_sum.astype(jnp.bfloat16))


def solution(mesh):
    placed = (P("ctx", "head"), P("ctx", None), P("ctx", None), P("head", "ctx"), P("ctx", "head"))
    return jax.shard_map(
        per_device,
        mesh=mesh,
        in_specs=placed,
        out_specs=(P("ctx", "head"), P(("ctx", "head"), None), P(("ctx", "head"), None)),
        check_vma=False,
    )
```

```python
import jax
import jax.numpy as jnp
from jax import lax
from jax.sharding import PartitionSpec as P


PARTNER_MASKS = {64: {4: 6, 32: 56}}


def scan_both(decay, state, grad, axis):
    devices, mine = lax.axis_size(axis), lax.axis_index(axis)
    block_decay, block_state, block_grad = decay, state, grad
    prefix_decay, prefix_state = jnp.ones_like(decay), jnp.zeros_like(state)
    suffix_decay, suffix_grad = jnp.ones_like(decay), jnp.zeros_like(grad)
    rows = state.shape[0]
    shift = 1
    while shift < devices:
        mask = PARTNER_MASKS.get(devices, {}).get(shift, shift)
        pairs = [(i, i ^ mask) for i in range(devices)]
        later = (mine & shift) != 0
        last = shift * 2 >= devices
        if last:
            message = jnp.concatenate(
                [block_decay[None, :], jnp.where(later, block_grad, block_state)], axis=0
            )
            got = lax.ppermute(message, axis, pairs)
            got_decay, got_state, got_grad = got[0], got[1:], got[1:]
        else:
            message = jnp.concatenate([block_decay[None, :], block_state, block_grad], axis=0)
            got = lax.ppermute(message, axis, pairs)
            got_decay, got_state, got_grad = got[0], got[1 : rows + 1], got[rows + 1 :]
        prefix_state = jnp.where(later, prefix_decay[None, :] * got_state + prefix_state, prefix_state)
        prefix_decay = jnp.where(later, got_decay * prefix_decay, prefix_decay)
        suffix_grad = jnp.where(later, suffix_grad, suffix_decay[None, :] * got_grad + suffix_grad)
        suffix_decay = jnp.where(later, suffix_decay, got_decay * suffix_decay)
        shift *= 2
        if not last:
            block_state = jnp.where(
                later,
                block_decay[None, :] * got_state + block_state,
                got_decay[None, :] * block_state + got_state,
            )
            block_grad = jnp.where(
                later,
                got_decay[None, :] * block_grad + got_grad,
                block_decay[None, :] * got_grad + block_grad,
            )
            block_decay = got_decay * block_decay
    return prefix_state, suffix_grad


def scatter_sum(values, axis):
    devices = lax.axis_size(axis)
    rows, cols = values.shape
    got = lax.all_to_all(values.reshape(devices, rows // devices, cols), axis, 0, 0)
    return jnp.sum(got, axis=0)


def heads_scaled(values, factor):
    head_count, length = factor.shape
    shaped = values.astype(jnp.float32).reshape(length, head_count, -1) * factor.T[:, :, None]
    return shaped.astype(jnp.bfloat16).reshape(length, -1)


def per_device(head_inputs, write_keys, read_queries, log_decay, out_grad):
    length, feature_width = head_inputs.shape
    head_count = log_decay.shape[0]
    head_size = feature_width // head_count
    upper = (jnp.arange(length)[:, None] <= jnp.arange(length)[None, :]).astype(jnp.float32)
    cumulative = jnp.dot(log_decay, upper, precision=lax.Precision.HIGHEST)
    block_end = cumulative[:, -1:]
    forward_w = jnp.exp(block_end - cumulative)
    backward_w = jnp.exp(cumulative)
    weighted_inputs = heads_scaled(head_inputs, forward_w)
    weighted_grads = heads_scaled(out_grad, backward_w)
    through = jnp.repeat(jnp.exp(block_end[:, 0]), head_size)
    own_state = jnp.dot(write_keys.T, weighted_inputs, preferred_element_type=jnp.float32)
    own_grad = jnp.dot(read_queries.T, weighted_grads, preferred_element_type=jnp.float32)

    entry, exit_ = scan_both(through, own_state, own_grad, "ctx")
    entry_bf = entry.astype(jnp.bfloat16)
    exit_bf = exit_.astype(jnp.bfloat16)

    causal = jnp.arange(length)[:, None] >= jnp.arange(length)[None, :]
    spread = cumulative[:, :, None] - cumulative[:, None, :]
    decay_mat = jnp.exp(jnp.where(causal[None], spread, -jnp.inf))
    scores = jnp.dot(read_queries, write_keys.T, preferred_element_type=jnp.float32)
    mixing = (scores[None] * decay_mat).astype(jnp.bfloat16)
    inputs_heads = head_inputs.reshape(length, head_count, head_size)
    grads_heads = out_grad.reshape(length, head_count, head_size)
    input_mix = jnp.einsum(
        "hts,thp->shp", mixing, grads_heads, preferred_element_type=jnp.float32
    )
    pair_grad = jnp.einsum(
        "thp,shp->hts", grads_heads, inputs_heads, preferred_element_type=jnp.float32
    )
    score_grad = jnp.sum(pair_grad * decay_mat, axis=0)
    write_mix = jnp.dot(
        score_grad.T, read_queries.astype(jnp.float32), precision=lax.Precision.HIGHEST
    )
    read_mix = jnp.dot(
        score_grad, write_keys.astype(jnp.float32), precision=lax.Precision.HIGHEST
    )

    input_state = (
        jnp.dot(write_keys, exit_bf, preferred_element_type=jnp.float32).reshape(
            length, head_count, head_size
        )
        * forward_w.T[:, :, None]
    )
    input_grad = (input_mix + input_state).astype(jnp.bfloat16).reshape(length, feature_width)
    write_state = jnp.dot(weighted_inputs, exit_bf.T, preferred_element_type=jnp.float32)
    read_state = jnp.dot(weighted_grads, entry_bf.T, preferred_element_type=jnp.float32)
    both = jnp.concatenate([write_mix + write_state, read_mix + read_state], axis=1)
    summed = scatter_sum(both, "head")
    states = write_keys.shape[1]
    write_sum, read_sum = summed[:, :states], summed[:, states:]
    return (input_grad, write_sum.astype(jnp.bfloat16), read_sum.astype(jnp.bfloat16))


def solution(mesh):
    placed = (P("ctx", "head"), P("ctx", None), P("ctx", None), P("head", "ctx"), P("ctx", "head"))
    return jax.shard_map(
        per_device,
        mesh=mesh,
        in_specs=placed,
        out_specs=(P("ctx", "head"), P(("ctx", "head"), None), P(("ctx", "head"), None)),
        check_vma=False,
    )
```

```python
import jax
import jax.numpy as jnp
from jax import lax
from jax.sharding import PartitionSpec as P


PARTNER_MASKS = {64: {4: 6, 32: 56}}


def scan_both(decay, state, grad, axis):
    devices, mine = lax.axis_size(axis), lax.axis_index(axis)
    block_decay, block_state, block_grad = decay, state, grad
    prefix_decay, prefix_state = jnp.ones_like(decay), jnp.zeros_like(state)
    suffix_decay, suffix_grad = jnp.ones_like(decay), jnp.zeros_like(grad)
    rows = state.shape[0]
    shift = 1
    while shift < devices:
        mask = PARTNER_MASKS.get(devices, {}).get(shift, shift)
        pairs = [(i, i ^ mask) for i in range(devices)]
        later = (mine & shift) != 0
        last = shift * 2 >= devices
        if last:
            message = jnp.concatenate(
                [block_decay[None, :], jnp.where(later, block_grad, block_state)], axis=0
            )
            got = lax.ppermute(message, axis, pairs)
            got_decay, got_state, got_grad = got[0], got[1:], got[1:]
        else:
            message = jnp.concatenate([block_decay[None, :], block_state, block_grad], axis=0)
            got = lax.ppermute(message, axis, pairs)
            got_decay, got_state, got_grad = got[0], got[1 : rows + 1], got[rows + 1 :]
        prefix_state = jnp.where(later, prefix_decay[None, :] * got_state + prefix_state, prefix_state)
        prefix_decay = jnp.where(later, got_decay * prefix_decay, prefix_decay)
        suffix_grad = jnp.where(later, suffix_grad, suffix_decay[None, :] * got_grad + suffix_grad)
        suffix_decay = jnp.where(later, suffix_decay, got_decay * suffix_decay)
        shift *= 2
        if not last:
            block_state = jnp.where(
                later,
                block_decay[None, :] * got_state + block_state,
                got_decay[None, :] * block_state + got_state,
            )
            block_grad = jnp.where(
                later,
                got_decay[None, :] * block_grad + got_grad,
                block_decay[None, :] * got_grad + block_grad,
            )
            block_decay = got_decay * block_decay
    return prefix_state, suffix_grad


def scatter_sum(values, axis):
    devices = lax.axis_size(axis)
    rows, cols = values.shape
    got = lax.all_to_all(values.reshape(devices, rows // devices, cols), axis, 0, 0)
    return jnp.sum(got, axis=0)


def heads_scaled(values, factor):
    head_count, length = factor.shape
    shaped = values.astype(jnp.float32).reshape(length, head_count, -1) * factor.T[:, :, None]
    return shaped.astype(jnp.bfloat16).reshape(length, -1)


def per_device(head_inputs, write_keys, read_queries, log_decay, out_grad):
    length, feature_width = head_inputs.shape
    head_count = log_decay.shape[0]
    head_size = feature_width // head_count
    cumulative = jnp.cumsum(log_decay, axis=1)
    block_end = cumulative[:, -1:]
    forward_w = jnp.exp(block_end - cumulative)
    backward_w = jnp.exp(cumulative)
    weighted_inputs = heads_scaled(head_inputs, forward_w)
    weighted_grads = heads_scaled(out_grad, backward_w)
    through = jnp.repeat(jnp.exp(block_end[:, 0]), head_size)
    own_state, own_grad = jnp.einsum(
        "kpn,kpc->knc",
        jnp.stack([write_keys, read_queries]),
        jnp.stack([weighted_inputs, weighted_grads]),
        preferred_element_type=jnp.float32,
    )

    entry, exit_ = scan_both(through, own_state, own_grad, "ctx")
    entry_bf = entry.astype(jnp.bfloat16)
    exit_bf = exit_.astype(jnp.bfloat16)

    causal = jnp.arange(length)[:, None] >= jnp.arange(length)[None, :]
    spread = cumulative[:, :, None] - cumulative[:, None, :]
    decay_mat = jnp.exp(jnp.where(causal[None], spread, -jnp.inf))
    scores = jnp.dot(read_queries, write_keys.T, preferred_element_type=jnp.float32)
    mixing = (scores[None] * decay_mat).astype(jnp.bfloat16)
    inputs_heads = head_inputs.reshape(length, head_count, head_size)
    grads_heads = out_grad.reshape(length, head_count, head_size)
    input_mix = jnp.einsum(
        "hts,thp->shp", mixing, grads_heads, preferred_element_type=jnp.float32
    )
    pair_grad = jnp.einsum(
        "thp,shp->hts", grads_heads, inputs_heads, preferred_element_type=jnp.float32
    )
    score_grad = jnp.sum(pair_grad * decay_mat, axis=0)
    write_mix = jnp.dot(
        score_grad.T, read_queries.astype(jnp.float32), precision=lax.Precision.HIGHEST
    )
    read_mix = jnp.dot(
        score_grad, write_keys.astype(jnp.float32), precision=lax.Precision.HIGHEST
    )

    input_state = (
        jnp.dot(write_keys, exit_bf, preferred_element_type=jnp.float32).reshape(
            length, head_count, head_size
        )
        * forward_w.T[:, :, None]
    )
    input_grad = (input_mix + input_state).astype(jnp.bfloat16).reshape(length, feature_width)
    write_state = jnp.dot(weighted_inputs, exit_bf.T, preferred_element_type=jnp.float32)
    read_state = jnp.dot(weighted_grads, entry_bf.T, preferred_element_type=jnp.float32)
    both = jnp.concatenate([write_mix + write_state, read_mix + read_state], axis=1)
    summed = scatter_sum(both, "head")
    states = write_keys.shape[1]
    write_sum, read_sum = summed[:, :states], summed[:, states:]
    return (input_grad, write_sum.astype(jnp.bfloat16), read_sum.astype(jnp.bfloat16))


def solution(mesh):
    placed = (P("ctx", "head"), P("ctx", None), P("ctx", None), P("head", "ctx"), P("ctx", "head"))
    return jax.shard_map(
        per_device,
        mesh=mesh,
        in_specs=placed,
        out_specs=(P("ctx", "head"), P(("ctx", "head"), None), P(("ctx", "head"), None)),
        check_vma=False,
    )
```

```python
import jax
import jax.numpy as jnp
from jax import lax
from jax.sharding import PartitionSpec as P


PARTNER_MASKS = {64: {4: 6, 32: 56}}


def scan_both(decay, state, grad, axis):
    devices, mine = lax.axis_size(axis), lax.axis_index(axis)
    block_decay, block_state, block_grad = decay, state, grad
    prefix_decay, prefix_state = jnp.ones_like(decay), jnp.zeros_like(state)
    suffix_decay, suffix_grad = jnp.ones_like(decay), jnp.zeros_like(grad)
    rows = state.shape[0]
    shift = 1
    while shift < devices:
        mask = PARTNER_MASKS.get(devices, {}).get(shift, shift)
        pairs = [(i, i ^ mask) for i in range(devices)]
        later = (mine & shift) != 0
        last = shift * 2 >= devices
        if last:
            message = jnp.concatenate(
                [block_decay[None, :], jnp.where(later, block_grad, block_state)], axis=0
            )
            got = lax.ppermute(message, axis, pairs)
            got_decay, got_state, got_grad = got[0], got[1:], got[1:]
        else:
            message = jnp.concatenate([block_decay[None, :], block_state, block_grad], axis=0)
            got = lax.ppermute(message, axis, pairs)
            got_decay, got_state, got_grad = got[0], got[1 : rows + 1], got[rows + 1 :]
        prefix_state = jnp.where(later, prefix_decay[None, :] * got_state + prefix_state, prefix_state)
        prefix_decay = jnp.where(later, got_decay * prefix_decay, prefix_decay)
        suffix_grad = jnp.where(later, suffix_grad, suffix_decay[None, :] * got_grad + suffix_grad)
        suffix_decay = jnp.where(later, suffix_decay, got_decay * suffix_decay)
        shift *= 2
        if not last:
            block_state = jnp.where(
                later,
                block_decay[None, :] * got_state + block_state,
                got_decay[None, :] * block_state + got_state,
            )
            block_grad = jnp.where(
                later,
                got_decay[None, :] * block_grad + got_grad,
                block_decay[None, :] * got_grad + block_grad,
            )
            block_decay = got_decay * block_decay
    return prefix_state, suffix_grad


def scatter_sum(values, axis):
    devices = lax.axis_size(axis)
    rows, cols = values.shape
    got = lax.all_to_all(values.reshape(devices, rows // devices, cols), axis, 0, 0)
    return jnp.sum(got, axis=0)


def heads_scaled(values, factor):
    head_count, length = factor.shape
    shaped = values.astype(jnp.float32).reshape(length, head_count, -1) * factor.T[:, :, None]
    return shaped.astype(jnp.bfloat16).reshape(length, -1)


def per_device(head_inputs, write_keys, read_queries, log_decay, out_grad):
    length, feature_width = head_inputs.shape
    states = write_keys.shape[1]
    packed = lax.optimization_barrier(
        jnp.concatenate([head_inputs, out_grad, write_keys, read_queries], axis=1)
    )
    head_inputs, out_grad, write_keys, read_queries = jnp.split(
        packed, [feature_width, 2 * feature_width, 2 * feature_width + states], axis=1
    )
    head_count = log_decay.shape[0]
    head_size = feature_width // head_count
    cumulative = jnp.cumsum(log_decay, axis=1)
    block_end = cumulative[:, -1:]
    forward_w = jnp.exp(block_end - cumulative)
    backward_w = jnp.exp(cumulative)
    weighted_inputs = heads_scaled(head_inputs, forward_w)
    weighted_grads = heads_scaled(out_grad, backward_w)
    through = jnp.repeat(jnp.exp(block_end[:, 0]), head_size)
    own_state, own_grad = jnp.einsum(
        "kpn,kpc->knc",
        jnp.stack([write_keys, read_queries]),
        jnp.stack([weighted_inputs, weighted_grads]),
        preferred_element_type=jnp.float32,
    )

    entry, exit_ = scan_both(through, own_state, own_grad, "ctx")
    entry_bf = entry.astype(jnp.bfloat16)
    exit_bf = exit_.astype(jnp.bfloat16)

    causal = jnp.arange(length)[:, None] >= jnp.arange(length)[None, :]
    spread = cumulative[:, :, None] - cumulative[:, None, :]
    decay_mat = jnp.exp(jnp.where(causal[None], spread, -jnp.inf))
    scores = jnp.dot(read_queries, write_keys.T, preferred_element_type=jnp.float32)
    mixing = (scores[None] * decay_mat).astype(jnp.bfloat16)
    inputs_heads = head_inputs.reshape(length, head_count, head_size)
    grads_heads = out_grad.reshape(length, head_count, head_size)
    input_mix = jnp.einsum(
        "hts,thp->shp", mixing, grads_heads, preferred_element_type=jnp.float32
    )
    pair_grad = jnp.einsum(
        "thp,shp->hts", grads_heads, inputs_heads, preferred_element_type=jnp.float32
    )
    score_grad = jnp.sum(pair_grad * decay_mat, axis=0)
    write_mix = jnp.dot(
        score_grad.T, read_queries.astype(jnp.float32), precision=lax.Precision.HIGHEST
    )
    read_mix = jnp.dot(
        score_grad, write_keys.astype(jnp.float32), precision=lax.Precision.HIGHEST
    )

    input_state = (
        jnp.dot(write_keys, exit_bf, preferred_element_type=jnp.float32).reshape(
            length, head_count, head_size
        )
        * forward_w.T[:, :, None]
    )
    input_grad = (input_mix + input_state).astype(jnp.bfloat16).reshape(length, feature_width)
    write_state = jnp.dot(weighted_inputs, exit_bf.T, preferred_element_type=jnp.float32)
    read_state = jnp.dot(weighted_grads, entry_bf.T, preferred_element_type=jnp.float32)
    both = jnp.concatenate([write_mix + write_state, read_mix + read_state], axis=1)
    summed = scatter_sum(both, "head")
    write_sum, read_sum = summed[:, :states], summed[:, states:]
    return (input_grad, write_sum.astype(jnp.bfloat16), read_sum.astype(jnp.bfloat16))


def solution(mesh):
    placed = (P("ctx", "head"), P("ctx", None), P("ctx", None), P("head", "ctx"), P("ctx", "head"))
    return jax.shard_map(
        per_device,
        mesh=mesh,
        in_specs=placed,
        out_specs=(P("ctx", "head"), P(("ctx", "head"), None), P(("ctx", "head"), None)),
        check_vma=False,
    )
```

```python
import jax
import jax.numpy as jnp
from jax import lax
from jax.sharding import PartitionSpec as P


PARTNER_MASKS = {64: {4: 6, 32: 56}}


def scan_both(decay, state, grad, axis):
    devices, mine = lax.axis_size(axis), lax.axis_index(axis)
    block_decay, block_state, block_grad = decay, state, grad
    prefix_decay, prefix_state = jnp.ones_like(decay), jnp.zeros_like(state)
    suffix_decay, suffix_grad = jnp.ones_like(decay), jnp.zeros_like(grad)
    rows = state.shape[0]
    shift = 1
    while shift < devices:
        mask = PARTNER_MASKS.get(devices, {}).get(shift, shift)
        pairs = [(i, i ^ mask) for i in range(devices)]
        later = (mine & shift) != 0
        last = shift * 2 >= devices
        if last:
            message = jnp.concatenate(
                [block_decay[None, :], jnp.where(later, block_grad, block_state)], axis=0
            )
            got = lax.ppermute(message, axis, pairs)
            got_decay, got_state, got_grad = got[0], got[1:], got[1:]
        else:
            message = jnp.concatenate([block_decay[None, :], block_state, block_grad], axis=0)
            got = lax.ppermute(message, axis, pairs)
            got_decay, got_state, got_grad = got[0], got[1 : rows + 1], got[rows + 1 :]
        prefix_state = jnp.where(later, prefix_decay[None, :] * got_state + prefix_state, prefix_state)
        prefix_decay = jnp.where(later, got_decay * prefix_decay, prefix_decay)
        suffix_grad = jnp.where(later, suffix_grad, suffix_decay[None, :] * got_grad + suffix_grad)
        suffix_decay = jnp.where(later, suffix_decay, got_decay * suffix_decay)
        shift *= 2
        if not last:
            block_state = jnp.where(
                later,
                block_decay[None, :] * got_state + block_state,
                got_decay[None, :] * block_state + got_state,
            )
            block_grad = jnp.where(
                later,
                got_decay[None, :] * block_grad + got_grad,
                block_decay[None, :] * got_grad + block_grad,
            )
            block_decay = got_decay * block_decay
    return prefix_state, suffix_grad


def scatter_sum(values, axis):
    devices = lax.axis_size(axis)
    rows, cols = values.shape
    got = lax.all_to_all(values.reshape(devices, rows // devices, cols), axis, 0, 0)
    return jnp.sum(got, axis=0)


def heads_scaled(values, factor):
    head_count, length = factor.shape
    shaped = values.astype(jnp.float32).reshape(length, head_count, -1) * factor.T[:, :, None]
    return shaped.astype(jnp.bfloat16).reshape(length, -1)


def per_device(head_inputs, write_keys, read_queries, log_decay, out_grad):
    length, feature_width = head_inputs.shape
    states = write_keys.shape[1]
    packed = lax.optimization_barrier(
        jnp.concatenate([head_inputs, out_grad, write_keys, read_queries], axis=1)
    )
    head_inputs, out_grad, write_keys, read_queries = jnp.split(
        packed, [feature_width, 2 * feature_width, 2 * feature_width + states], axis=1
    )
    head_count = log_decay.shape[0]
    head_size = feature_width // head_count
    cumulative, reach = log_decay, 1
    while reach < length:
        cumulative = cumulative + jnp.pad(cumulative[:, :-reach], ((0, 0), (reach, 0)))
        reach *= 2
    block_end = cumulative[:, -1:]
    forward_w = jnp.exp(block_end - cumulative)
    backward_w = jnp.exp(cumulative)
    weighted_inputs = heads_scaled(head_inputs, forward_w)
    weighted_grads = heads_scaled(out_grad, backward_w)
    through = jnp.repeat(jnp.exp(block_end[:, 0]), head_size)
    own_state, own_grad = jnp.einsum(
        "kpn,kpc->knc",
        jnp.stack([write_keys, read_queries]),
        jnp.stack([weighted_inputs, weighted_grads]),
        preferred_element_type=jnp.float32,
    )

    entry, exit_ = scan_both(through, own_state, own_grad, "ctx")
    entry_bf = entry.astype(jnp.bfloat16)
    exit_bf = exit_.astype(jnp.bfloat16)

    causal = jnp.arange(length)[:, None] >= jnp.arange(length)[None, :]
    spread = cumulative[:, :, None] - cumulative[:, None, :]
    decay_mat = jnp.exp(jnp.where(causal[None], spread, -jnp.inf))
    scores = jnp.dot(read_queries, write_keys.T, preferred_element_type=jnp.float32)
    mixing = (scores[None] * decay_mat).astype(jnp.bfloat16)
    inputs_heads = head_inputs.reshape(length, head_count, head_size)
    grads_heads = out_grad.reshape(length, head_count, head_size)
    input_mix = jnp.einsum(
        "hts,thp->shp", mixing, grads_heads, preferred_element_type=jnp.float32
    )
    pair_grad = jnp.einsum(
        "thp,shp->hts", grads_heads, inputs_heads, preferred_element_type=jnp.float32
    )
    score_grad = jnp.sum(pair_grad * decay_mat, axis=0)
    write_mix = jnp.dot(
        score_grad.T, read_queries.astype(jnp.float32), precision=lax.Precision.HIGHEST
    )
    read_mix = jnp.dot(
        score_grad, write_keys.astype(jnp.float32), precision=lax.Precision.HIGHEST
    )

    input_state = (
        jnp.dot(write_keys, exit_bf, preferred_element_type=jnp.float32).reshape(
            length, head_count, head_size
        )
        * forward_w.T[:, :, None]
    )
    input_grad = (input_mix + input_state).astype(jnp.bfloat16).reshape(length, feature_width)
    write_state = jnp.dot(weighted_inputs, exit_bf.T, preferred_element_type=jnp.float32)
    read_state = jnp.dot(weighted_grads, entry_bf.T, preferred_element_type=jnp.float32)
    both = jnp.concatenate([write_mix + write_state, read_mix + read_state], axis=1)
    summed = scatter_sum(both, "head")
    write_sum, read_sum = summed[:, :states], summed[:, states:]
    return (input_grad, write_sum.astype(jnp.bfloat16), read_sum.astype(jnp.bfloat16))


def solution(mesh):
    placed = (P("ctx", "head"), P("ctx", None), P("ctx", None), P("head", "ctx"), P("ctx", "head"))
    return jax.shard_map(
        per_device,
        mesh=mesh,
        in_specs=placed,
        out_specs=(P("ctx", "head"), P(("ctx", "head"), None), P(("ctx", "head"), None)),
        check_vma=False,
    )
```

```python
import jax
import jax.numpy as jnp
from jax import lax
from jax.sharding import PartitionSpec as P


PARTNER_MASKS = {64: {4: 6, 32: 56}}


def scan_both(decay, state, grad, axis):
    devices, mine = lax.axis_size(axis), lax.axis_index(axis)
    block_decay, block_state, block_grad = decay, state, grad
    prefix_decay, prefix_state = jnp.ones_like(decay), jnp.zeros_like(state)
    suffix_decay, suffix_grad = jnp.ones_like(decay), jnp.zeros_like(grad)
    rows = state.shape[0]
    shift = 1
    while shift < devices:
        mask = PARTNER_MASKS.get(devices, {}).get(shift, shift)
        pairs = [(i, i ^ mask) for i in range(devices)]
        later = (mine & shift) != 0
        last = shift * 2 >= devices
        if last:
            message = jnp.concatenate(
                [jnp.where(later, block_grad, block_state), block_decay[None, :]], axis=0
            )
            got = lax.ppermute(message, axis, pairs)
            got_decay, got_state, got_grad = got[rows], got[:rows], got[:rows]
        else:
            message = jnp.concatenate([block_state, block_grad, block_decay[None, :]], axis=0)
            got = lax.ppermute(message, axis, pairs)
            got_decay, got_state, got_grad = got[2 * rows], got[:rows], got[rows : 2 * rows]
        prefix_state = jnp.where(later, prefix_decay[None, :] * got_state + prefix_state, prefix_state)
        prefix_decay = jnp.where(later, got_decay * prefix_decay, prefix_decay)
        suffix_grad = jnp.where(later, suffix_grad, suffix_decay[None, :] * got_grad + suffix_grad)
        suffix_decay = jnp.where(later, suffix_decay, got_decay * suffix_decay)
        shift *= 2
        if not last:
            block_state = jnp.where(
                later,
                block_decay[None, :] * got_state + block_state,
                got_decay[None, :] * block_state + got_state,
            )
            block_grad = jnp.where(
                later,
                got_decay[None, :] * block_grad + got_grad,
                block_decay[None, :] * got_grad + block_grad,
            )
            block_decay = got_decay * block_decay
    return prefix_state, suffix_grad


def scatter_sum(values, axis):
    devices = lax.axis_size(axis)
    rows, cols = values.shape
    got = lax.all_to_all(values.reshape(devices, rows // devices, cols), axis, 0, 0)
    return jnp.sum(got, axis=0)


def heads_scaled(values, factor):
    head_count, length = factor.shape
    shaped = values.astype(jnp.float32).reshape(length, head_count, -1) * factor.T[:, :, None]
    return shaped.astype(jnp.bfloat16).reshape(length, -1)


def per_device(head_inputs, write_keys, read_queries, log_decay, out_grad):
    length, feature_width = head_inputs.shape
    states = write_keys.shape[1]
    packed = lax.optimization_barrier(
        jnp.concatenate([head_inputs, out_grad, write_keys, read_queries], axis=1)
    )
    head_inputs, out_grad, write_keys, read_queries = jnp.split(
        packed, [feature_width, 2 * feature_width, 2 * feature_width + states], axis=1
    )
    head_count = log_decay.shape[0]
    head_size = feature_width // head_count
    cumulative = jnp.cumsum(log_decay, axis=1)
    block_end = cumulative[:, -1:]
    forward_w = jnp.exp(block_end - cumulative)
    backward_w = jnp.exp(cumulative)
    weighted_inputs = heads_scaled(head_inputs, forward_w)
    weighted_grads = heads_scaled(out_grad, backward_w)
    through = jnp.repeat(jnp.exp(block_end[:, 0]), head_size)
    own_state, own_grad = jnp.einsum(
        "kpn,kpc->knc",
        jnp.stack([write_keys, read_queries]),
        jnp.stack([weighted_inputs, weighted_grads]),
        preferred_element_type=jnp.float32,
    )

    entry, exit_ = scan_both(through, own_state, own_grad, "ctx")
    entry_bf = entry.astype(jnp.bfloat16)
    exit_bf = exit_.astype(jnp.bfloat16)

    causal = jnp.arange(length)[:, None] >= jnp.arange(length)[None, :]
    spread = cumulative[:, :, None] - cumulative[:, None, :]
    decay_mat = jnp.exp(jnp.where(causal[None], spread, -jnp.inf))
    scores = jnp.dot(read_queries, write_keys.T, preferred_element_type=jnp.float32)
    mixing = (scores[None] * decay_mat).astype(jnp.bfloat16)
    inputs_heads = head_inputs.reshape(length, head_count, head_size)
    grads_heads = out_grad.reshape(length, head_count, head_size)
    input_mix = jnp.einsum(
        "hts,thp->shp", mixing, grads_heads, preferred_element_type=jnp.float32
    )
    pair_grad = jnp.einsum(
        "thp,shp->hts", grads_heads, inputs_heads, preferred_element_type=jnp.float32
    )
    score_grad = jnp.sum(pair_grad * decay_mat, axis=0)
    write_mix = jnp.dot(
        score_grad.T, read_queries.astype(jnp.float32), precision=lax.Precision.HIGHEST
    )
    read_mix = jnp.dot(
        score_grad, write_keys.astype(jnp.float32), precision=lax.Precision.HIGHEST
    )

    input_state = (
        jnp.dot(write_keys, exit_bf, preferred_element_type=jnp.float32).reshape(
            length, head_count, head_size
        )
        * forward_w.T[:, :, None]
    )
    input_grad = (input_mix + input_state).astype(jnp.bfloat16).reshape(length, feature_width)
    write_state = jnp.dot(weighted_inputs, exit_bf.T, preferred_element_type=jnp.float32)
    read_state = jnp.dot(weighted_grads, entry_bf.T, preferred_element_type=jnp.float32)
    both = jnp.concatenate([write_mix + write_state, read_mix + read_state], axis=1)
    summed = scatter_sum(both, "head")
    write_sum, read_sum = summed[:, :states], summed[:, states:]
    return (input_grad, write_sum.astype(jnp.bfloat16), read_sum.astype(jnp.bfloat16))


def solution(mesh):
    placed = (P("ctx", "head"), P("ctx", None), P("ctx", None), P("head", "ctx"), P("ctx", "head"))
    return jax.shard_map(
        per_device,
        mesh=mesh,
        in_specs=placed,
        out_specs=(P("ctx", "head"), P(("ctx", "head"), None), P(("ctx", "head"), None)),
        check_vma=False,
    )
```

```python
import jax
import jax.numpy as jnp
from jax import lax
from jax.sharding import PartitionSpec as P


PARTNER_MASKS = {16: {4: 6}}


def joined(earlier, later):
    a1, s1, g1 = earlier
    a2, s2, g2 = later
    return (a1 * a2, a2[None, :] * s1 + s2, a1[None, :] * g2 + g1)


def chosen(flag, yes, no):
    return tuple(jnp.where(flag, y, n) for y, n in zip(yes, no))


def scan_both(decay, state, grad, low_axis, high_axis):
    devices, mine = lax.axis_size(low_axis), lax.axis_index(low_axis)
    rows = state.shape[0]
    identity = (jnp.ones_like(decay), jnp.zeros_like(state), jnp.zeros_like(grad))
    block = (decay, state, grad)
    prefix, suffix = identity, identity
    shift = 1
    while shift < devices:
        mask = PARTNER_MASKS.get(devices, {}).get(shift, shift)
        pairs = [(i, i ^ mask) for i in range(devices)]
        later = (mine & shift) != 0
        message = jnp.concatenate([block[1], block[2], block[0][None, :]], axis=0)
        got = lax.ppermute(message, low_axis, pairs)
        piece = (got[2 * rows], got[:rows], got[rows : 2 * rows])
        prefix = chosen(later, joined(piece, prefix), prefix)
        suffix = chosen(later, suffix, joined(suffix, piece))
        block = chosen(later, joined(piece, block), joined(block, piece))
        shift *= 2
    size, place = lax.axis_size(high_axis), lax.axis_index(high_axis)
    message = jnp.concatenate([block[1], block[2], block[0][None, :]], axis=0)
    got = lax.all_to_all(jnp.broadcast_to(message[None], (size,) + message.shape), high_axis, 0, 0)
    before, after = identity, identity
    for member in range(size):
        piece = (got[member, 2 * rows], got[member, :rows], got[member, rows : 2 * rows])
        before = chosen(member < place, joined(before, piece), before)
        after = chosen(member > place, joined(after, piece), after)
    prefix = joined(before, prefix)
    suffix = joined(suffix, after)
    return prefix[1], suffix[2]


def scatter_sum(values, axis):
    devices = lax.axis_size(axis)
    rows, cols = values.shape
    got = lax.all_to_all(values.reshape(devices, rows // devices, cols), axis, 0, 0)
    return jnp.sum(got, axis=0)


def heads_scaled(values, factor):
    head_count, length = factor.shape
    shaped = values.astype(jnp.float32).reshape(length, head_count, -1) * factor.T[:, :, None]
    return shaped.astype(jnp.bfloat16).reshape(length, -1)


def per_device(head_inputs, write_keys, read_queries, log_decay, out_grad):
    length, feature_width = head_inputs.shape
    states = write_keys.shape[1]
    packed = lax.optimization_barrier(
        jnp.concatenate([head_inputs, out_grad, write_keys, read_queries], axis=1)
    )
    head_inputs, out_grad, write_keys, read_queries = jnp.split(
        packed, [feature_width, 2 * feature_width, 2 * feature_width + states], axis=1
    )
    head_count = log_decay.shape[0]
    head_size = feature_width // head_count
    cumulative = jnp.cumsum(log_decay, axis=1)
    block_end = cumulative[:, -1:]
    forward_w = jnp.exp(block_end - cumulative)
    backward_w = jnp.exp(cumulative)
    weighted_inputs = heads_scaled(head_inputs, forward_w)
    weighted_grads = heads_scaled(out_grad, backward_w)
    through = jnp.repeat(jnp.exp(block_end[:, 0]), head_size)
    own_state, own_grad = jnp.einsum(
        "kpn,kpc->knc",
        jnp.stack([write_keys, read_queries]),
        jnp.stack([weighted_inputs, weighted_grads]),
        preferred_element_type=jnp.float32,
    )

    entry, exit_ = scan_both(through, own_state, own_grad, "ctx_lo", "ctx_hi")
    entry_bf = entry.astype(jnp.bfloat16)
    exit_bf = exit_.astype(jnp.bfloat16)

    causal = jnp.arange(length)[:, None] >= jnp.arange(length)[None, :]
    spread = cumulative[:, :, None] - cumulative[:, None, :]
    decay_mat = jnp.exp(jnp.where(causal[None], spread, -jnp.inf))
    scores = jnp.dot(read_queries, write_keys.T, preferred_element_type=jnp.float32)
    mixing = (scores[None] * decay_mat).astype(jnp.bfloat16)
    inputs_heads = head_inputs.reshape(length, head_count, head_size)
    grads_heads = out_grad.reshape(length, head_count, head_size)
    input_mix = jnp.einsum(
        "hts,thp->shp", mixing, grads_heads, preferred_element_type=jnp.float32
    )
    pair_grad = jnp.einsum(
        "thp,shp->hts", grads_heads, inputs_heads, preferred_element_type=jnp.float32
    )
    score_grad = jnp.sum(pair_grad * decay_mat, axis=0)
    write_mix = jnp.dot(
        score_grad.T, read_queries.astype(jnp.float32), precision=lax.Precision.HIGHEST
    )
    read_mix = jnp.dot(
        score_grad, write_keys.astype(jnp.float32), precision=lax.Precision.HIGHEST
    )

    input_state = (
        jnp.dot(write_keys, exit_bf, preferred_element_type=jnp.float32).reshape(
            length, head_count, head_size
        )
        * forward_w.T[:, :, None]
    )
    input_grad = (input_mix + input_state).astype(jnp.bfloat16).reshape(length, feature_width)
    write_state = jnp.dot(weighted_inputs, exit_bf.T, preferred_element_type=jnp.float32)
    read_state = jnp.dot(weighted_grads, entry_bf.T, preferred_element_type=jnp.float32)
    both = jnp.concatenate([write_mix + write_state, read_mix + read_state], axis=1)
    summed = scatter_sum(both, "head")
    write_sum, read_sum = summed[:, :states], summed[:, states:]
    return (input_grad, write_sum.astype(jnp.bfloat16), read_sum.astype(jnp.bfloat16))


def solution(mesh):
    ctx_size = mesh.shape["ctx"]
    hi = 4 if ctx_size % 4 == 0 and ctx_size >= 8 else 1
    split = jax.sharding.Mesh(
        mesh.devices.reshape(hi, ctx_size // hi, mesh.shape["head"]), ("ctx_hi", "ctx_lo", "head")
    )
    ctx = ("ctx_hi", "ctx_lo")
    placed = (P(ctx, "head"), P(ctx, None), P(ctx, None), P("head", ctx), P(ctx, "head"))
    return jax.shard_map(
        per_device,
        mesh=split,
        in_specs=placed,
        out_specs=(P(ctx, "head"), P(ctx + ("head",), None), P(ctx + ("head",), None)),
        check_vma=False,
    )
```

```python
import jax
import jax.numpy as jnp
from jax import lax
from jax.sharding import PartitionSpec as P


PARTNER_MASKS = {64: {4: 6, 32: 56}}


def scan_both(decay, state, grad, axis):
    devices, mine = lax.axis_size(axis), lax.axis_index(axis)
    block_decay, block_state, block_grad = decay, state, grad
    prefix_decay, prefix_state = jnp.ones_like(decay), jnp.zeros_like(state)
    suffix_decay, suffix_grad = jnp.ones_like(decay), jnp.zeros_like(grad)
    rows = state.shape[0]
    shift = 1
    while shift < devices:
        mask = PARTNER_MASKS.get(devices, {}).get(shift, shift)
        pairs = [(i, i ^ mask) for i in range(devices)]
        later = (mine & shift) != 0
        last = shift * 2 >= devices
        if last:
            got = lax.ppermute(jnp.where(later, block_grad, block_state), axis, pairs)
            got_decay, got_state, got_grad = None, got, got
        else:
            message = jnp.concatenate([block_state, block_grad, block_decay[None, :]], axis=0)
            got = lax.ppermute(message, axis, pairs)
            got_decay, got_state, got_grad = got[2 * rows], got[:rows], got[rows : 2 * rows]
        prefix_state = jnp.where(later, prefix_decay[None, :] * got_state + prefix_state, prefix_state)
        suffix_grad = jnp.where(later, suffix_grad, suffix_decay[None, :] * got_grad + suffix_grad)
        shift *= 2
        if not last:
            prefix_decay = jnp.where(later, got_decay * prefix_decay, prefix_decay)
            suffix_decay = jnp.where(later, suffix_decay, got_decay * suffix_decay)
            block_state = jnp.where(
                later,
                block_decay[None, :] * got_state + block_state,
                got_decay[None, :] * block_state + got_state,
            )
            block_grad = jnp.where(
                later,
                got_decay[None, :] * block_grad + got_grad,
                block_decay[None, :] * got_grad + block_grad,
            )
            block_decay = got_decay * block_decay
    return prefix_state, suffix_grad


def scatter_sum(values, axis):
    devices = lax.axis_size(axis)
    rows, cols = values.shape
    got = lax.all_to_all(values.reshape(devices, rows // devices, cols), axis, 0, 0)
    return jnp.sum(got, axis=0)


def heads_scaled(values, factor):
    head_count, length = factor.shape
    shaped = values.astype(jnp.float32).reshape(length, head_count, -1) * factor.T[:, :, None]
    return shaped.astype(jnp.bfloat16).reshape(length, -1)


def per_device(head_inputs, write_keys, read_queries, log_decay, out_grad):
    length, feature_width = head_inputs.shape
    states = write_keys.shape[1]
    packed = lax.optimization_barrier(
        jnp.concatenate([head_inputs, out_grad, write_keys, read_queries], axis=1)
    )
    head_inputs, out_grad, write_keys, read_queries = jnp.split(
        packed, [feature_width, 2 * feature_width, 2 * feature_width + states], axis=1
    )
    head_count = log_decay.shape[0]
    head_size = feature_width // head_count
    cumulative = jnp.cumsum(log_decay, axis=1)
    block_end = cumulative[:, -1:]
    forward_w = jnp.exp(block_end - cumulative)
    backward_w = jnp.exp(cumulative)
    weighted_inputs = heads_scaled(head_inputs, forward_w)
    weighted_grads = heads_scaled(out_grad, backward_w)
    through = jnp.repeat(jnp.exp(block_end[:, 0]), head_size)
    own_state, own_grad = jnp.einsum(
        "kpn,kpc->knc",
        jnp.stack([write_keys, read_queries]),
        jnp.stack([weighted_inputs, weighted_grads]),
        preferred_element_type=jnp.float32,
    )

    entry, exit_ = scan_both(through, own_state, own_grad, "ctx")
    entry_bf = entry.astype(jnp.bfloat16)
    exit_bf = exit_.astype(jnp.bfloat16)

    causal = jnp.arange(length)[:, None] >= jnp.arange(length)[None, :]
    spread = cumulative[:, :, None] - cumulative[:, None, :]
    decay_mat = jnp.exp(jnp.where(causal[None], spread, -jnp.inf))
    scores = jnp.dot(read_queries, write_keys.T, preferred_element_type=jnp.float32)
    mixing = (scores[None] * decay_mat).astype(jnp.bfloat16)
    inputs_heads = head_inputs.reshape(length, head_count, head_size)
    grads_heads = out_grad.reshape(length, head_count, head_size)
    input_mix = jnp.einsum(
        "hts,thp->shp", mixing, grads_heads, preferred_element_type=jnp.float32
    )
    pair_grad = jnp.einsum(
        "thp,shp->hts", grads_heads, inputs_heads, preferred_element_type=jnp.float32
    )
    score_grad = jnp.sum(pair_grad * decay_mat, axis=0)
    write_mix = jnp.dot(
        score_grad.T, read_queries.astype(jnp.float32), precision=lax.Precision.HIGHEST
    )
    read_mix = jnp.dot(
        score_grad, write_keys.astype(jnp.float32), precision=lax.Precision.HIGHEST
    )

    input_state = (
        jnp.dot(write_keys, exit_bf, preferred_element_type=jnp.float32).reshape(
            length, head_count, head_size
        )
        * forward_w.T[:, :, None]
    )
    input_grad = (input_mix + input_state).astype(jnp.bfloat16).reshape(length, feature_width)
    write_state = jnp.dot(weighted_inputs, exit_bf.T, preferred_element_type=jnp.float32)
    read_state = jnp.dot(weighted_grads, entry_bf.T, preferred_element_type=jnp.float32)
    both = jnp.concatenate([write_mix + write_state, read_mix + read_state], axis=1)
    summed = scatter_sum(both, "head")
    write_sum, read_sum = summed[:, :states], summed[:, states:]
    return (input_grad, write_sum.astype(jnp.bfloat16), read_sum.astype(jnp.bfloat16))


def solution(mesh):
    placed = (P("ctx", "head"), P("ctx", None), P("ctx", None), P("head", "ctx"), P("ctx", "head"))
    return jax.shard_map(
        per_device,
        mesh=mesh,
        in_specs=placed,
        out_specs=(P("ctx", "head"), P(("ctx", "head"), None), P(("ctx", "head"), None)),
        check_vma=False,
    )
```

```python
import jax
import jax.numpy as jnp
from jax import lax
from jax.sharding import PartitionSpec as P


PARTNER_MASKS = {64: {4: 6, 16: 24, 32: 56}}


def scan_both(decay, state, grad, axis):
    devices, mine = lax.axis_size(axis), lax.axis_index(axis)
    block_decay, block_state, block_grad = decay, state, grad
    prefix_decay, prefix_state = jnp.ones_like(decay), jnp.zeros_like(state)
    suffix_decay, suffix_grad = jnp.ones_like(decay), jnp.zeros_like(grad)
    rows = state.shape[0]
    shift = 1
    while shift < devices:
        mask = PARTNER_MASKS.get(devices, {}).get(shift, shift)
        pairs = [(i, i ^ mask) for i in range(devices)]
        later = (mine & shift) != 0
        last = shift * 2 >= devices
        if last:
            got = lax.ppermute(jnp.where(later, block_grad, block_state), axis, pairs)
            got_decay, got_state, got_grad = None, got, got
        else:
            message = jnp.concatenate([block_state, block_grad, block_decay[None, :]], axis=0)
            got = lax.ppermute(message, axis, pairs)
            got_decay, got_state, got_grad = got[2 * rows], got[:rows], got[rows : 2 * rows]
        prefix_state = jnp.where(later, prefix_decay[None, :] * got_state + prefix_state, prefix_state)
        suffix_grad = jnp.where(later, suffix_grad, suffix_decay[None, :] * got_grad + suffix_grad)
        shift *= 2
        if not last:
            prefix_decay = jnp.where(later, got_decay * prefix_decay, prefix_decay)
            suffix_decay = jnp.where(later, suffix_decay, got_decay * suffix_decay)
            block_state = jnp.where(
                later,
                block_decay[None, :] * got_state + block_state,
                got_decay[None, :] * block_state + got_state,
            )
            block_grad = jnp.where(
                later,
                got_decay[None, :] * block_grad + got_grad,
                block_decay[None, :] * got_grad + block_grad,
            )
            block_decay = got_decay * block_decay
    return prefix_state, suffix_grad


def scatter_sum(values, axis):
    devices = lax.axis_size(axis)
    rows, cols = values.shape
    got = lax.all_to_all(values.reshape(devices, rows // devices, cols), axis, 0, 0)
    return jnp.sum(got, axis=0)


def heads_scaled(values, factor):
    head_count, length = factor.shape
    shaped = values.astype(jnp.float32).reshape(length, head_count, -1) * factor.T[:, :, None]
    return shaped.astype(jnp.bfloat16).reshape(length, -1)


def per_device(head_inputs, write_keys, read_queries, log_decay, out_grad):
    length, feature_width = head_inputs.shape
    states = write_keys.shape[1]
    packed = lax.optimization_barrier(
        jnp.concatenate([head_inputs, out_grad, write_keys, read_queries], axis=1)
    )
    head_inputs, out_grad, write_keys, read_queries = jnp.split(
        packed, [feature_width, 2 * feature_width, 2 * feature_width + states], axis=1
    )
    head_count = log_decay.shape[0]
    head_size = feature_width // head_count
    cumulative = jnp.cumsum(log_decay, axis=1)
    block_end = cumulative[:, -1:]
    forward_w = jnp.exp(block_end - cumulative)
    backward_w = jnp.exp(cumulative)
    weighted_inputs = heads_scaled(head_inputs, forward_w)
    weighted_grads = heads_scaled(out_grad, backward_w)
    through = jnp.repeat(jnp.exp(block_end[:, 0]), head_size)
    own_state, own_grad = jnp.einsum(
        "kpn,kpc->knc",
        jnp.stack([write_keys, read_queries]),
        jnp.stack([weighted_inputs, weighted_grads]),
        preferred_element_type=jnp.float32,
    )

    entry, exit_ = scan_both(through, own_state, own_grad, "ctx")
    entry_bf = entry.astype(jnp.bfloat16)
    exit_bf = exit_.astype(jnp.bfloat16)

    causal = jnp.arange(length)[:, None] >= jnp.arange(length)[None, :]
    spread = cumulative[:, :, None] - cumulative[:, None, :]
    decay_mat = jnp.exp(jnp.where(causal[None], spread, -jnp.inf))
    scores = jnp.dot(read_queries, write_keys.T, preferred_element_type=jnp.float32)
    mixing = (scores[None] * decay_mat).astype(jnp.bfloat16)
    inputs_heads = head_inputs.reshape(length, head_count, head_size)
    grads_heads = out_grad.reshape(length, head_count, head_size)
    input_mix = jnp.einsum(
        "hts,thp->shp", mixing, grads_heads, preferred_element_type=jnp.float32
    )
    pair_grad = jnp.einsum(
        "thp,shp->hts", grads_heads, inputs_heads, preferred_element_type=jnp.float32
    )
    score_grad = jnp.sum(pair_grad * decay_mat, axis=0)
    write_mix = jnp.dot(
        score_grad.T, read_queries.astype(jnp.float32), precision=lax.Precision.HIGHEST
    )
    read_mix = jnp.dot(
        score_grad, write_keys.astype(jnp.float32), precision=lax.Precision.HIGHEST
    )

    input_state = (
        jnp.dot(write_keys, exit_bf, preferred_element_type=jnp.float32).reshape(
            length, head_count, head_size
        )
        * forward_w.T[:, :, None]
    )
    input_grad = (input_mix + input_state).astype(jnp.bfloat16).reshape(length, feature_width)
    write_state = jnp.dot(weighted_inputs, exit_bf.T, preferred_element_type=jnp.float32)
    read_state = jnp.dot(weighted_grads, entry_bf.T, preferred_element_type=jnp.float32)
    both = jnp.concatenate([write_mix + write_state, read_mix + read_state], axis=1)
    summed = scatter_sum(both, "head")
    write_sum, read_sum = summed[:, :states], summed[:, states:]
    return (input_grad, write_sum.astype(jnp.bfloat16), read_sum.astype(jnp.bfloat16))


def solution(mesh):
    placed = (P("ctx", "head"), P("ctx", None), P("ctx", None), P("head", "ctx"), P("ctx", "head"))
    return jax.shard_map(
        per_device,
        mesh=mesh,
        in_specs=placed,
        out_specs=(P("ctx", "head"), P(("ctx", "head"), None), P(("ctx", "head"), None)),
        check_vma=False,
    )
```

```python
import jax
import jax.numpy as jnp
from jax import lax
from jax.sharding import PartitionSpec as P


PARTNER_MASKS = {64: {4: 6, 16: 24, 32: 48}}


def scan_both(decay, state, grad, axis):
    devices, mine = lax.axis_size(axis), lax.axis_index(axis)
    block_decay, block_state, block_grad = decay, state, grad
    prefix_decay, prefix_state = jnp.ones_like(decay), jnp.zeros_like(state)
    suffix_decay, suffix_grad = jnp.ones_like(decay), jnp.zeros_like(grad)
    rows = state.shape[0]
    shift = 1
    while shift < devices:
        mask = PARTNER_MASKS.get(devices, {}).get(shift, shift)
        pairs = [(i, i ^ mask) for i in range(devices)]
        later = (mine & shift) != 0
        last = shift * 2 >= devices
        if last:
            got = lax.ppermute(jnp.where(later, block_grad, block_state), axis, pairs)
            got_decay, got_state, got_grad = None, got, got
        else:
            message = jnp.concatenate([block_state, block_grad, block_decay[None, :]], axis=0)
            got = lax.ppermute(message, axis, pairs)
            got_decay, got_state, got_grad = got[2 * rows], got[:rows], got[rows : 2 * rows]
        prefix_state = jnp.where(later, prefix_decay[None, :] * got_state + prefix_state, prefix_state)
        suffix_grad = jnp.where(later, suffix_grad, suffix_decay[None, :] * got_grad + suffix_grad)
        shift *= 2
        if not last:
            prefix_decay = jnp.where(later, got_decay * prefix_decay, prefix_decay)
            suffix_decay = jnp.where(later, suffix_decay, got_decay * suffix_decay)
            block_state = jnp.where(
                later,
                block_decay[None, :] * got_state + block_state,
                got_decay[None, :] * block_state + got_state,
            )
            block_grad = jnp.where(
                later,
                got_decay[None, :] * block_grad + got_grad,
                block_decay[None, :] * got_grad + block_grad,
            )
            block_decay = got_decay * block_decay
    return prefix_state, suffix_grad


def scatter_sum(values, axis):
    devices = lax.axis_size(axis)
    rows, cols = values.shape
    got = lax.all_to_all(values.reshape(devices, rows // devices, cols), axis, 0, 0)
    return jnp.sum(got, axis=0)


def heads_scaled(values, factor):
    head_count, length = factor.shape
    shaped = values.astype(jnp.float32).reshape(length, head_count, -1) * factor.T[:, :, None]
    return shaped.astype(jnp.bfloat16).reshape(length, -1)


def per_device(head_inputs, write_keys, read_queries, log_decay, out_grad):
    length, feature_width = head_inputs.shape
    states = write_keys.shape[1]
    packed = lax.optimization_barrier(
        jnp.concatenate([head_inputs, out_grad, write_keys, read_queries], axis=1)
    )
    head_inputs, out_grad, write_keys, read_queries = jnp.split(
        packed, [feature_width, 2 * feature_width, 2 * feature_width + states], axis=1
    )
    head_count = log_decay.shape[0]
    head_size = feature_width // head_count
    cumulative = jnp.cumsum(log_decay, axis=1)
    block_end = cumulative[:, -1:]
    forward_w = jnp.exp(block_end - cumulative)
    backward_w = jnp.exp(cumulative)
    weighted_inputs = heads_scaled(head_inputs, forward_w)
    weighted_grads = heads_scaled(out_grad, backward_w)
    through = jnp.repeat(jnp.exp(block_end[:, 0]), head_size)
    own_state, own_grad = jnp.einsum(
        "kpn,kpc->knc",
        jnp.stack([write_keys, read_queries]),
        jnp.stack([weighted_inputs, weighted_grads]),
        preferred_element_type=jnp.float32,
    )

    entry, exit_ = scan_both(through, own_state, own_grad, "ctx")
    entry_bf = entry.astype(jnp.bfloat16)
    exit_bf = exit_.astype(jnp.bfloat16)

    causal = jnp.arange(length)[:, None] >= jnp.arange(length)[None, :]
    spread = cumulative[:, :, None] - cumulative[:, None, :]
    decay_mat = jnp.exp(jnp.where(causal[None], spread, -jnp.inf))
    scores = jnp.dot(read_queries, write_keys.T, preferred_element_type=jnp.float32)
    mixing = (scores[None] * decay_mat).astype(jnp.bfloat16)
    inputs_heads = head_inputs.reshape(length, head_count, head_size)
    grads_heads = out_grad.reshape(length, head_count, head_size)
    input_mix = jnp.einsum(
        "hts,thp->shp", mixing, grads_heads, preferred_element_type=jnp.float32
    )
    pair_grad = jnp.einsum(
        "thp,shp->hts", grads_heads, inputs_heads, preferred_element_type=jnp.float32
    )
    score_grad = jnp.sum(pair_grad * decay_mat, axis=0)
    write_mix = jnp.dot(
        score_grad.T, read_queries.astype(jnp.float32), precision=lax.Precision.HIGHEST
    )
    read_mix = jnp.dot(
        score_grad, write_keys.astype(jnp.float32), precision=lax.Precision.HIGHEST
    )

    input_state = (
        jnp.dot(write_keys, exit_bf, preferred_element_type=jnp.float32).reshape(
            length, head_count, head_size
        )
        * forward_w.T[:, :, None]
    )
    input_grad = (input_mix + input_state).astype(jnp.bfloat16).reshape(length, feature_width)
    write_state = jnp.dot(weighted_inputs, exit_bf.T, preferred_element_type=jnp.float32)
    read_state = jnp.dot(weighted_grads, entry_bf.T, preferred_element_type=jnp.float32)
    both = jnp.concatenate([write_mix + write_state, read_mix + read_state], axis=1)
    summed = scatter_sum(both, "head")
    write_sum, read_sum = summed[:, :states], summed[:, states:]
    return (input_grad, write_sum.astype(jnp.bfloat16), read_sum.astype(jnp.bfloat16))


def solution(mesh):
    placed = (P("ctx", "head"), P("ctx", None), P("ctx", None), P("head", "ctx"), P("ctx", "head"))
    return jax.shard_map(
        per_device,
        mesh=mesh,
        in_specs=placed,
        out_specs=(P("ctx", "head"), P(("ctx", "head"), None), P(("ctx", "head"), None)),
        check_vma=False,
    )
```

```python
import jax
import jax.numpy as jnp
from jax import lax
from jax.sharding import PartitionSpec as P


PARTNER_MASKS = {64: {4: 6, 8: 14, 16: 24, 32: 56}}


def scan_both(decay, state, grad, axis):
    devices, mine = lax.axis_size(axis), lax.axis_index(axis)
    block_decay, block_state, block_grad = decay, state, grad
    prefix_decay, prefix_state = jnp.ones_like(decay), jnp.zeros_like(state)
    suffix_decay, suffix_grad = jnp.ones_like(decay), jnp.zeros_like(grad)
    rows = state.shape[0]
    shift = 1
    while shift < devices:
        mask = PARTNER_MASKS.get(devices, {}).get(shift, shift)
        pairs = [(i, i ^ mask) for i in range(devices)]
        later = (mine & shift) != 0
        last = shift * 2 >= devices
        if last:
            got = lax.ppermute(jnp.where(later, block_grad, block_state), axis, pairs)
            got_decay, got_state, got_grad = None, got, got
        else:
            message = jnp.concatenate([block_state, block_grad, block_decay[None, :]], axis=0)
            got = lax.ppermute(message, axis, pairs)
            got_decay, got_state, got_grad = got[2 * rows], got[:rows], got[rows : 2 * rows]
        prefix_state = jnp.where(later, prefix_decay[None, :] * got_state + prefix_state, prefix_state)
        suffix_grad = jnp.where(later, suffix_grad, suffix_decay[None, :] * got_grad + suffix_grad)
        shift *= 2
        if not last:
            prefix_decay = jnp.where(later, got_decay * prefix_decay, prefix_decay)
            suffix_decay = jnp.where(later, suffix_decay, got_decay * suffix_decay)
            block_state = jnp.where(
                later,
                block_decay[None, :] * got_state + block_state,
                got_decay[None, :] * block_state + got_state,
            )
            block_grad = jnp.where(
                later,
                got_decay[None, :] * block_grad + got_grad,
                block_decay[None, :] * got_grad + block_grad,
            )
            block_decay = got_decay * block_decay
    return prefix_state, suffix_grad


def scatter_sum(values, axis):
    devices = lax.axis_size(axis)
    rows, cols = values.shape
    got = lax.all_to_all(values.reshape(devices, rows // devices, cols), axis, 0, 0)
    return jnp.sum(got, axis=0)


def heads_scaled(values, factor):
    head_count, length = factor.shape
    shaped = values.astype(jnp.float32).reshape(length, head_count, -1) * factor.T[:, :, None]
    return shaped.astype(jnp.bfloat16).reshape(length, -1)


def per_device(head_inputs, write_keys, read_queries, log_decay, out_grad):
    length, feature_width = head_inputs.shape
    states = write_keys.shape[1]
    packed = lax.optimization_barrier(
        jnp.concatenate([head_inputs, out_grad, write_keys, read_queries], axis=1)
    )
    head_inputs, out_grad, write_keys, read_queries = jnp.split(
        packed, [feature_width, 2 * feature_width, 2 * feature_width + states], axis=1
    )
    head_count = log_decay.shape[0]
    head_size = feature_width // head_count
    cumulative = jnp.cumsum(log_decay, axis=1)
    block_end = cumulative[:, -1:]
    forward_w = jnp.exp(block_end - cumulative)
    backward_w = jnp.exp(cumulative)
    weighted_inputs = heads_scaled(head_inputs, forward_w)
    weighted_grads = heads_scaled(out_grad, backward_w)
    through = jnp.repeat(jnp.exp(block_end[:, 0]), head_size)
    own_state, own_grad = jnp.einsum(
        "kpn,kpc->knc",
        jnp.stack([write_keys, read_queries]),
        jnp.stack([weighted_inputs, weighted_grads]),
        preferred_element_type=jnp.float32,
    )

    entry, exit_ = scan_both(through, own_state, own_grad, "ctx")
    entry_bf = entry.astype(jnp.bfloat16)
    exit_bf = exit_.astype(jnp.bfloat16)

    causal = jnp.arange(length)[:, None] >= jnp.arange(length)[None, :]
    spread = cumulative[:, :, None] - cumulative[:, None, :]
    decay_mat = jnp.exp(jnp.where(causal[None], spread, -jnp.inf))
    scores = jnp.dot(read_queries, write_keys.T, preferred_element_type=jnp.float32)
    mixing = (scores[None] * decay_mat).astype(jnp.bfloat16)
    inputs_heads = head_inputs.reshape(length, head_count, head_size)
    grads_heads = out_grad.reshape(length, head_count, head_size)
    input_mix = jnp.einsum(
        "hts,thp->shp", mixing, grads_heads, preferred_element_type=jnp.float32
    )
    pair_grad = jnp.einsum(
        "thp,shp->hts", grads_heads, inputs_heads, preferred_element_type=jnp.float32
    )
    score_grad = jnp.sum(pair_grad * decay_mat, axis=0)
    write_mix = jnp.dot(
        score_grad.T, read_queries.astype(jnp.float32), precision=lax.Precision.HIGHEST
    )
    read_mix = jnp.dot(
        score_grad, write_keys.astype(jnp.float32), precision=lax.Precision.HIGHEST
    )

    input_state = (
        jnp.dot(write_keys, exit_bf, preferred_element_type=jnp.float32).reshape(
            length, head_count, head_size
        )
        * forward_w.T[:, :, None]
    )
    input_grad = (input_mix + input_state).astype(jnp.bfloat16).reshape(length, feature_width)
    write_state = jnp.dot(weighted_inputs, exit_bf.T, preferred_element_type=jnp.float32)
    read_state = jnp.dot(weighted_grads, entry_bf.T, preferred_element_type=jnp.float32)
    both = jnp.concatenate([write_mix + write_state, read_mix + read_state], axis=1)
    summed = scatter_sum(both, "head")
    write_sum, read_sum = summed[:, :states], summed[:, states:]
    return (input_grad, write_sum.astype(jnp.bfloat16), read_sum.astype(jnp.bfloat16))


def solution(mesh):
    placed = (P("ctx", "head"), P("ctx", None), P("ctx", None), P("head", "ctx"), P("ctx", "head"))
    return jax.shard_map(
        per_device,
        mesh=mesh,
        in_specs=placed,
        out_specs=(P("ctx", "head"), P(("ctx", "head"), None), P(("ctx", "head"), None)),
        check_vma=False,
    )
```

```python
import jax
import jax.numpy as jnp
from jax import lax
from jax.sharding import PartitionSpec as P


PARTNER_MASKS = {64: {16: 24, 32: 56}}


def scan_both(decay, state, grad, axis):
    devices, mine = lax.axis_size(axis), lax.axis_index(axis)
    block_decay, block_state, block_grad = decay, state, grad
    prefix_decay, prefix_state = jnp.ones_like(decay), jnp.zeros_like(state)
    suffix_decay, suffix_grad = jnp.ones_like(decay), jnp.zeros_like(grad)
    rows = state.shape[0]
    shift = 1
    while shift < devices:
        mask = PARTNER_MASKS.get(devices, {}).get(shift, shift)
        pairs = [(i, i ^ mask) for i in range(devices)]
        later = (mine & shift) != 0
        last = shift * 2 >= devices
        if last:
            got = lax.ppermute(jnp.where(later, block_grad, block_state), axis, pairs)
            got_decay, got_state, got_grad = None, got, got
        else:
            message = jnp.concatenate([block_state, block_grad, block_decay[None, :]], axis=0)
            got = lax.ppermute(message, axis, pairs)
            got_decay, got_state, got_grad = got[2 * rows], got[:rows], got[rows : 2 * rows]
        prefix_state = jnp.where(later, prefix_decay[None, :] * got_state + prefix_state, prefix_state)
        suffix_grad = jnp.where(later, suffix_grad, suffix_decay[None, :] * got_grad + suffix_grad)
        shift *= 2
        if not last:
            prefix_decay = jnp.where(later, got_decay * prefix_decay, prefix_decay)
            suffix_decay = jnp.where(later, suffix_decay, got_decay * suffix_decay)
            block_state = jnp.where(
                later,
                block_decay[None, :] * got_state + block_state,
                got_decay[None, :] * block_state + got_state,
            )
            block_grad = jnp.where(
                later,
                got_decay[None, :] * block_grad + got_grad,
                block_decay[None, :] * got_grad + block_grad,
            )
            block_decay = got_decay * block_decay
    return prefix_state, suffix_grad


def scatter_sum(values, axis):
    devices = lax.axis_size(axis)
    rows, cols = values.shape
    got = lax.all_to_all(values.reshape(devices, rows // devices, cols), axis, 0, 0)
    return jnp.sum(got, axis=0)


def heads_scaled(values, factor):
    head_count, length = factor.shape
    shaped = values.astype(jnp.float32).reshape(length, head_count, -1) * factor.T[:, :, None]
    return shaped.astype(jnp.bfloat16).reshape(length, -1)


def per_device(head_inputs, write_keys, read_queries, log_decay, out_grad):
    length, feature_width = head_inputs.shape
    states = write_keys.shape[1]
    packed = lax.optimization_barrier(
        jnp.concatenate([head_inputs, out_grad, write_keys, read_queries], axis=1)
    )
    head_inputs, out_grad, write_keys, read_queries = jnp.split(
        packed, [feature_width, 2 * feature_width, 2 * feature_width + states], axis=1
    )
    head_count = log_decay.shape[0]
    head_size = feature_width // head_count
    cumulative = jnp.cumsum(log_decay, axis=1)
    block_end = cumulative[:, -1:]
    forward_w = jnp.exp(block_end - cumulative)
    backward_w = jnp.exp(cumulative)
    weighted_inputs = heads_scaled(head_inputs, forward_w)
    weighted_grads = heads_scaled(out_grad, backward_w)
    through = jnp.repeat(jnp.exp(block_end[:, 0]), head_size)
    own_state, own_grad = jnp.einsum(
        "kpn,kpc->knc",
        jnp.stack([write_keys, read_queries]),
        jnp.stack([weighted_inputs, weighted_grads]),
        preferred_element_type=jnp.float32,
    )

    entry, exit_ = scan_both(through, own_state, own_grad, "ctx")
    entry_bf = entry.astype(jnp.bfloat16)
    exit_bf = exit_.astype(jnp.bfloat16)

    causal = jnp.arange(length)[:, None] >= jnp.arange(length)[None, :]
    spread = cumulative[:, :, None] - cumulative[:, None, :]
    decay_mat = jnp.exp(jnp.where(causal[None], spread, -jnp.inf))
    scores = jnp.dot(read_queries, write_keys.T, preferred_element_type=jnp.float32)
    mixing = (scores[None] * decay_mat).astype(jnp.bfloat16)
    inputs_heads = head_inputs.reshape(length, head_count, head_size)
    grads_heads = out_grad.reshape(length, head_count, head_size)
    input_mix = jnp.einsum(
        "hts,thp->shp", mixing, grads_heads, preferred_element_type=jnp.float32
    )
    pair_grad = jnp.einsum(
        "thp,shp->hts", grads_heads, inputs_heads, preferred_element_type=jnp.float32
    )
    score_grad = jnp.sum(pair_grad * decay_mat, axis=0)
    write_mix = jnp.dot(
        score_grad.T, read_queries.astype(jnp.float32), precision=lax.Precision.HIGHEST
    )
    read_mix = jnp.dot(
        score_grad, write_keys.astype(jnp.float32), precision=lax.Precision.HIGHEST
    )

    input_state = (
        jnp.dot(write_keys, exit_bf, preferred_element_type=jnp.float32).reshape(
            length, head_count, head_size
        )
        * forward_w.T[:, :, None]
    )
    input_grad = (input_mix + input_state).astype(jnp.bfloat16).reshape(length, feature_width)
    write_state = jnp.dot(weighted_inputs, exit_bf.T, preferred_element_type=jnp.float32)
    read_state = jnp.dot(weighted_grads, entry_bf.T, preferred_element_type=jnp.float32)
    both = jnp.concatenate([write_mix + write_state, read_mix + read_state], axis=1)
    summed = scatter_sum(both, "head")
    write_sum, read_sum = summed[:, :states], summed[:, states:]
    return (input_grad, write_sum.astype(jnp.bfloat16), read_sum.astype(jnp.bfloat16))


def solution(mesh):
    placed = (P("ctx", "head"), P("ctx", None), P("ctx", None), P("head", "ctx"), P("ctx", "head"))
    return jax.shard_map(
        per_device,
        mesh=mesh,
        in_specs=placed,
        out_specs=(P("ctx", "head"), P(("ctx", "head"), None), P(("ctx", "head"), None)),
        check_vma=False,
    )
```
